256 devices in a mesh: head: 8 (over y, core), tile: 32 (over x, z).
Axes of the slice: x: 4, y: 4, z: 8, core: 2. Of those that a mesh axis runs over, the one named last changes fastest.
Arguments:
- query: bfloat16 [32768, 3072], P(('tile', 'head')), may hold values from -8 to 8
- key: bfloat16 [32768, 3072], P(('tile', 'head')), may hold values from -8 to 8
- value: bfloat16 [32768, 3072], P(('tile', 'head')), may hold values from -6 to 6
- grad_out: bfloat16 [32768, 3072], P(('tile', 'head')), may hold values from -6 to 6
- block_mask: int32 [256, 256], replicated, may hold values from 0 to 1, as said below
- tile_order: int32 [256], replicated, may hold values from 0 to 255, as said below
Outputs:
- attn_out: bfloat16 [32768, 3072], P(('tile', 'head'))
- grad_query: bfloat16 [32768, 3072], P(('tile', 'head'))
- grad_key: bfloat16 [32768, 3072], P(('tile', 'head'))
- grad_value: bfloat16 [32768, 3072], P(('tile', 'head'))
The draws below stay inside these ranges and needn't reach their ends.
Inputs may be any that keep to these rules, and one draw needn't show every extreme that they name: block_mask[a, b] is 1 only where clip tiles a and b differ by at most one in frame, grid row and grid column; every diagonal entry is 1; a row has at most 9 ones, and some row has exactly 9. A permutation that keeps every tile in its frame: tile_order[s] // 8 == s // 8.
All inputs are finite; a program needn't handle non-finite values.
Results may differ from the reference program's by a relative error of at most 0.022.
Values may be sent and summed in bfloat16 or wider, within the bound.
No kernel may reach another device: no remote copies, remote signals or barrier semaphores. Data moves between devices by JAX's collectives and lax.ppermute only.
A program may use at most 192 MiB of HBM per device.

```python
import jax
import jax.numpy as jnp
from jax import lax

HD = 128
HEADS = 24
TILE = 128
PLANE = 8
TOKENS = 32768
MAXK = 9
N_HEAD = 8
N_TILE = 32


def clip_grid():
    tile_count = N_HEAD * N_TILE
    grid_cols = N_HEAD // 2
    index_all = jnp.arange(tile_count, dtype=jnp.int32)
    frame_of = index_all // N_HEAD
    row_of = index_all % N_HEAD // grid_cols
    col_of = index_all % grid_cols
    return (index_all, frame_of, row_of, col_of)


def draw_block_mask(key, part):
    index_all, frame_of, row_of, col_of = clip_grid()
    tile_count = N_HEAD * N_TILE
    within = (jnp.abs(frame_of[:, None] - frame_of[None, :]) <= 1) & (jnp.abs(row_of[:, None] - row_of[None, :]) <= 1) & (jnp.abs(col_of[:, None] - col_of[None, :]) <= 1)
    window_count = jnp.sum(within.astype(jnp.int32), axis=1)
    diagonal = index_all[:, None] == index_all[None, :]
    priority = jax.random.randint(jax.random.fold_in(key, 13), (tile_count, tile_count), 0, 1 << 16) * tile_count + index_all[None, :]
    priority = jnp.where(diagonal, 1 << 30, priority)
    priority = jnp.where(within, priority, -1)
    rank_in = jnp.sum(((priority[:, None, :] > priority[:, :, None]) & within[:, None, :]).astype(jnp.int32), axis=2)
    capped = within & (rank_in < MAXK)
    kept = jax.random.randint(jax.random.fold_in(key, 11), (tile_count, tile_count), 0, 10) < 8
    ranking = jax.random.randint(jax.random.fold_in(key, 12), (tile_count,), 0, 1 << 20) * tile_count + index_all
    ranking = jnp.where(window_count >= MAXK, ranking, -1)
    chosen = jnp.argmax(ranking)
    full_row = (index_all == chosen)[:, None]
    return (capped & (kept | diagonal | full_row)).astype(jnp.int32)


def shuffle_frame(frame_key):
    return jax.random.permutation(frame_key, N_HEAD)


def draw_tile_order(key, part):
    keys_frame = jax.random.split(jax.random.fold_in(key, 21), N_TILE)
    shuffled = jax.vmap(shuffle_frame)(keys_frame).astype(jnp.int32)
    offsets = jnp.arange(N_TILE, dtype=jnp.int32)[:, None] * N_HEAD
    return (shuffled + offsets).reshape(N_TILE * N_HEAD)


def draw_query(key, part):
    shape_all = (N_HEAD * N_TILE, TILE, HEADS, HD)
    values_all = jnp.clip(1.5 * jax.random.normal(jax.random.fold_in(key, 41), shape_all, jnp.float32), -8.0, 8.0)
    return values_all.reshape(TOKENS, HEADS * HD).astype(jnp.bfloat16)


def draw_key(key, part):
    shape_all = (N_HEAD * N_TILE, TILE, HEADS, HD)
    values_all = jnp.clip(1.5 * jax.random.normal(jax.random.fold_in(key, 42), shape_all, jnp.float32), -8.0, 8.0)
    return values_all.reshape(TOKENS, HEADS * HD).astype(jnp.bfloat16)


def block_scale(own_key, shape, shards, smallest, high):
    gain, own = 1.0, jax.random.fold_in(own_key, 6)
    for dim, parts in shards:
        draws = jnp.exp(jax.random.uniform(jax.random.fold_in(own, dim), (parts,), jnp.float32, smallest / len(shards), high / len(shards)))
        gain = gain * jnp.repeat(draws, shape[dim] // parts).reshape([-1 if axis == dim else 1 for axis in range(len(shape))])
    return gain


def centred(key, shape, deviation, most, shards=(), kind=jnp.bfloat16):
    factor_of = block_scale(key, shape, shards, -0.22, 0.18) if shards else 1.0
    result = jax.random.normal(key, shape, jnp.float32) * deviation * factor_of
    return jnp.minimum(jnp.maximum(result, -most), most).astype(kind)


def setup_inputs(seed: int = 0) -> dict:
    key_list = jax.random.split(jax.random.key(seed), 7)
    query = draw_query(jax.random.fold_in(key_list[6], 71), 0)
    key = draw_key(jax.random.fold_in(key_list[6], 71), 0)
    value = centred(key_list[2], (TOKENS, HEADS * HD), 1.0, 6.0, ((0, 256),))
    grad_out = centred(key_list[3], (TOKENS, HEADS * HD), 1.0, 6.0, ((0, 256),))
    block_mask = draw_block_mask(jax.random.fold_in(key_list[6], 71), 0)
    tile_order = draw_tile_order(jax.random.fold_in(key_list[6], 71), 0)
    return {"query": query, "key": key, "value": value, "grad_out": grad_out, "block_mask": block_mask, "tile_order": tile_order}


NEG = -1.0e30


def window_lists(block_mask, tile_order, frame_idx, frames, per_frame):
    tile_count = per_frame * frames
    query_clip = lax.dynamic_slice_in_dim(tile_order, (frame_idx * per_frame).astype(jnp.int32), per_frame)
    cand_slot = (frame_idx - 1) * per_frame + jnp.arange(3 * per_frame, dtype=jnp.int32)
    valid_slot = ((cand_slot >= 0) & (cand_slot < tile_count)).astype(jnp.int32)
    cand_clip = jnp.take(tile_order, jnp.clip(cand_slot, 0, tile_count - 1).astype(jnp.int32))
    forward_active = block_mask[query_clip[:, None], cand_clip[None, :]] * valid_slot[None, :]
    return forward_active


def compact_slots(forward_active, max_keys):
    slot_key = jnp.argsort(1 - forward_active, axis=1, stable=True)[:, :max_keys].astype(jnp.int32)
    live_slot = jnp.take_along_axis(forward_active, slot_key, axis=1) > 0
    return slot_key, live_slot


def reference(query, key, value, grad_out, block_mask, tile_order):
    rows_frame = PLANE * TILE
    width_all = HEADS * HD
    scaling = HD ** -0.5
    pad_rows = jnp.zeros((rows_frame, width_all), jnp.bfloat16)
    key_pad = jnp.concatenate([pad_rows, key, pad_rows], axis=0)
    value_pad = jnp.concatenate([pad_rows, value, pad_rows], axis=0)
    acc_zero = jnp.zeros((TOKENS + 2 * rows_frame, width_all), jnp.float32)

    def frame_step(carry, frame_idx):
        key_acc, value_acc = carry
        start = (frame_idx * rows_frame).astype(jnp.int32)
        q_f = lax.dynamic_slice_in_dim(query, start, rows_frame).astype(jnp.float32).reshape(PLANE, TILE, HEADS, HD)
        g_f = lax.dynamic_slice_in_dim(grad_out, start, rows_frame).astype(jnp.float32).reshape(PLANE, TILE, HEADS, HD)
        k_win = lax.dynamic_slice_in_dim(key_pad, start, 3 * rows_frame).astype(jnp.float32).reshape(3 * PLANE, TILE, HEADS, HD)
        v_win = lax.dynamic_slice_in_dim(value_pad, start, 3 * rows_frame).astype(jnp.float32).reshape(3 * PLANE, TILE, HEADS, HD)
        forward_active = window_lists(block_mask, tile_order, frame_idx, N_TILE, PLANE)
        slot_key, live_slot = compact_slots(forward_active, MAXK)
        key_blocks = jnp.take(k_win, slot_key, axis=0)
        value_blocks = jnp.take(v_win, slot_key, axis=0)
        scores = jnp.einsum('pqhd,pskhd->phqsk', q_f, key_blocks) * scaling
        scores = jnp.where(live_slot[:, None, None, :, None], scores, NEG)
        top = jnp.max(scores, axis=(3, 4), keepdims=True)
        log_total = top + jnp.log(jnp.sum(jnp.exp(scores - top), axis=(3, 4), keepdims=True))
        attn_prob = jnp.exp(scores - log_total)
        prob_bf = attn_prob.astype(jnp.bfloat16).astype(jnp.float32)
        output = jnp.einsum('phqsk,pskhd->pqhd', prob_bf, value_blocks).astype(jnp.bfloat16)
        delta = jnp.sum(g_f * output.astype(jnp.float32), axis=3)
        dprob = jnp.einsum('pqhd,pskhd->phqsk', g_f, value_blocks)
        delta_t = jnp.transpose(delta, (0, 2, 1))[:, :, :, None, None]
        dscore = (attn_prob * (dprob - delta_t)).astype(jnp.bfloat16).astype(jnp.float32)
        grad_q = (jnp.einsum('phqsk,pskhd->pqhd', dscore, key_blocks) * scaling).astype(jnp.bfloat16)
        key_terms = jnp.einsum('phqsk,pqhd->pskhd', dscore, q_f) * scaling
        value_terms = jnp.einsum('phqsk,pqhd->pskhd', prob_bf, g_f)
        onehot = (slot_key[:, :, None] == jnp.arange(3 * PLANE, dtype=jnp.int32)[None, None, :]).astype(jnp.float32)
        key_win_grad = jnp.einsum('psc,pskhd->ckhd', onehot, key_terms, precision=lax.Precision.HIGHEST).reshape(3 * rows_frame, width_all)
        value_win_grad = jnp.einsum('psc,pskhd->ckhd', onehot, value_terms, precision=lax.Precision.HIGHEST).reshape(3 * rows_frame, width_all)
        key_acc = lax.dynamic_update_slice_in_dim(key_acc, lax.dynamic_slice_in_dim(key_acc, start, 3 * rows_frame) + key_win_grad, start, 0)
        value_acc = lax.dynamic_update_slice_in_dim(value_acc, lax.dynamic_slice_in_dim(value_acc, start, 3 * rows_frame) + value_win_grad, start, 0)
        return (key_acc, value_acc), (output.reshape(rows_frame, width_all), grad_q.reshape(rows_frame, width_all))

    carry, stacked = lax.scan(frame_step, (acc_zero, acc_zero), jnp.arange(N_TILE, dtype=jnp.int32))
    key_acc, value_acc = carry
    outputs, grads = stacked
    attn_out = outputs.reshape(TOKENS, width_all)
    grad_query = grads.reshape(TOKENS, width_all)
    grad_key = key_acc[rows_frame:rows_frame + TOKENS].astype(jnp.bfloat16)
    grad_value = value_acc[rows_frame:rows_frame + TOKENS].astype(jnp.bfloat16)
    return (attn_out, grad_query, grad_key, grad_value)
```

```python
import jax
import jax.numpy as jnp
from jax import lax
from jax.sharding import PartitionSpec as P
from jax.experimental import pallas as pl
from jax.experimental.pallas import tpu as pltpu

HD = 128


NEG = -1e30


def with_halo(array, sides, width):
    for axis, dim in sides:
        size, length = (lax.axis_size(axis), array.shape[dim])
        up = [(i, (i + 1) % size) for i in range(size - 1)]
        down = [(j, i) for i, j in up]
        last = lax.slice_in_dim(array, length - width, length, axis=dim)
        initial = lax.slice_in_dim(array, 0, width, axis=dim)
        before = lax.ppermute(last, axis, up)
        after = lax.ppermute(initial, axis, down)
        array = jnp.concatenate([before, array, after], axis=dim)
    return array


def passed_along(value, axis, steps):
    count = lax.axis_size(axis)
    initial, last = (max(0, -steps), min(count, count - steps))
    return lax.ppermute(value, axis, [(source, source + steps) for source in range(initial, last)])


def window_lists(block_mask, tile_order, frame_idx, frames, per_frame):
    tile_count = per_frame * frames
    query_clip = lax.dynamic_slice_in_dim(tile_order, frame_idx * per_frame, per_frame)
    cand_slot = (frame_idx - 1) * per_frame + jnp.arange(3 * per_frame, dtype=jnp.int32)
    valid_slot = ((cand_slot >= 0) & (cand_slot < tile_count)).astype(jnp.int32)
    cand_clip = jnp.take(tile_order, jnp.clip(cand_slot, 0, tile_count - 1))
    forward_active = block_mask[query_clip[:, None], cand_clip[None, :]] * valid_slot[None, :]
    backward_active = block_mask[cand_clip[:, None], query_clip[None, :]] * valid_slot[:, None]
    return (forward_active, backward_active)


def compact_slots(forward_active, max_keys):
    slot_key = jnp.argsort(1 - forward_active, axis=1, stable=True)[:, :max_keys]
    live_slot = jnp.take_along_axis(forward_active, slot_key, axis=1) > 0
    return (slot_key, live_slot)


def attn_kernel(slot_ref, live_ref, q_ref, g_ref, k_ref, v_ref, o_ref, dq_ref, dk_ref, dv_ref, s_scr, p_scr):
    tile_rows = HD
    query_tiles, max_keys = slot_ref.shape
    scaling = HD ** (-0.5)
    dk_ref[...] = jnp.zeros(dk_ref.shape, dk_ref.dtype)
    dv_ref[...] = jnp.zeros(dv_ref.shape, dv_ref.dtype)
    nt = (((1,), (1,)), ((), ()))
    tn = (((0,), (0,)), ((), ()))

    def key_rows(p, s):
        return pl.ds(pl.multiple_of(slot_ref[p, s] * tile_rows, tile_rows), tile_rows)

    def body(p, carry):
        rows = pl.ds(pl.multiple_of(p * tile_rows, tile_rows), tile_rows)
        q = q_ref[rows, :]
        g = g_ref[rows, :]
        top = jnp.full((tile_rows, 1), NEG, jnp.float32)
        for s in range(max_keys):
            k = k_ref[key_rows(p, s), :]
            sc = lax.dot_general(q, k, nt, preferred_element_type=jnp.float32) * scaling
            sc = jnp.where(live_ref[p, s] > 0, sc, NEG)
            s_scr[s] = sc
            top = jnp.maximum(top, jnp.max(sc, axis=1, keepdims=True))
        total = jnp.zeros((tile_rows, 1), jnp.float32)
        for s in range(max_keys):
            total = total + jnp.sum(jnp.exp(s_scr[s] - top), axis=1, keepdims=True)
        log_total = top + jnp.log(total)
        out_acc = jnp.zeros((tile_rows, HD), jnp.float32)
        for s in range(max_keys):
            prob = jnp.exp(s_scr[s] - log_total)
            p_scr[s] = prob
            v = v_ref[key_rows(p, s), :]
            out_acc = out_acc + jnp.dot(
                prob.astype(jnp.bfloat16), v, preferred_element_type=jnp.float32
            )
        out = out_acc.astype(jnp.bfloat16)
        o_ref[rows, :] = out
        delta = jnp.sum(g.astype(jnp.float32) * out.astype(jnp.float32), axis=1, keepdims=True)
        dq_acc = jnp.zeros((tile_rows, HD), jnp.float32)
        for s in range(max_keys):
            krows = key_rows(p, s)
            k = k_ref[krows, :]
            v = v_ref[krows, :]
            prob = p_scr[s]
            dprob = lax.dot_general(g, v, nt, preferred_element_type=jnp.float32)
            dscore = (prob * (dprob - delta)).astype(jnp.bfloat16)
            dq_acc = dq_acc + jnp.dot(dscore, k, preferred_element_type=jnp.float32)
            dk_ref[krows, :] += (
                lax.dot_general(dscore, q, tn, preferred_element_type=jnp.float32) * scaling
            )
            dv_ref[krows, :] += lax.dot_general(
                prob.astype(jnp.bfloat16), g, tn, preferred_element_type=jnp.float32
            )
        dq_ref[rows, :] = (dq_acc * scaling).astype(dq_ref.dtype)
        return carry

    lax.fori_loop(0, query_tiles, body, 0)


def attention_heads(q_loc, g_loc, k_win, v_win, slot_key, live_slot):
    rows_frame, width = q_loc.shape
    window_rows = k_win.shape[0]
    query_tiles, max_keys = slot_key.shape
    head_count = width // HD
    row_spec = pl.BlockSpec((rows_frame, HD), lambda h, *_: (0, h))
    win_spec = pl.BlockSpec((window_rows, HD), lambda h, *_: (0, h))
    flops = 12 * query_tiles * max_keys * HD * HD * HD * head_count
    grid_spec = pltpu.PrefetchScalarGridSpec(
        num_scalar_prefetch=2,
        grid=(head_count,),
        in_specs=[row_spec, row_spec, win_spec, win_spec],
        out_specs=[row_spec, row_spec, win_spec, win_spec],
        scratch_shapes=[
            pltpu.VMEM((max_keys, HD, HD), jnp.float32),
            pltpu.VMEM((max_keys, HD, HD), jnp.float32),
        ],
    )
    return pl.pallas_call(
        attn_kernel,
        grid_spec=grid_spec,
        out_shape=[
            jax.ShapeDtypeStruct((rows_frame, width), jnp.bfloat16),
            jax.ShapeDtypeStruct((rows_frame, width), jnp.bfloat16),
            jax.ShapeDtypeStruct((window_rows, width), jnp.float32),
            jax.ShapeDtypeStruct((window_rows, width), jnp.float32),
        ],
        cost_estimate=pl.CostEstimate(
            flops=flops,
            transcendentals=2 * query_tiles * max_keys * HD * HD * head_count,
            bytes_accessed=2 * (4 * rows_frame + 2 * window_rows) * width + 8 * window_rows * width,
        ),
    )(slot_key, live_slot.astype(jnp.int32), q_loc, g_loc, k_win, v_win)


def local(query, key, value, grad_out, block_mask, tile_order):
    per_frame = lax.axis_size("head")
    frames = lax.axis_size("tile")
    frame_idx = lax.axis_index("tile")
    max_keys = 3 * min(3, per_frame // 2)
    tile_rows = query.shape[0]
    q_loc, k_loc, v_loc, g_loc = (
        lax.all_to_all(query, "head", split_axis=1, concat_axis=0, tiled=True),
        lax.all_to_all(key, "head", split_axis=1, concat_axis=0, tiled=True),
        lax.all_to_all(value, "head", split_axis=1, concat_axis=0, tiled=True),
        lax.all_to_all(grad_out, "head", split_axis=1, concat_axis=0, tiled=True),
    )
    width_dev = q_loc.shape[1]
    head_count = width_dev // HD
    rows_frame = per_frame * tile_rows
    scaling = HD ** (-0.5)
    kv_rims = with_halo(jnp.stack([k_loc, v_loc]), (("tile", 1),), rows_frame)
    forward_active, backward_active = window_lists(
        block_mask, tile_order, frame_idx, frames, per_frame
    )
    slot_key, live_slot = compact_slots(forward_active, max_keys)
    out_rows, dq_rows, key_grad_win, value_grad_win = attention_heads(
        q_loc, g_loc, kv_rims[0], kv_rims[1], slot_key, live_slot
    )
    grads_win = jnp.stack([key_grad_win, value_grad_win])
    middle = grads_win[:, rows_frame : 2 * rows_frame]
    lower_part = grads_win[:, :rows_frame]
    upper_part = grads_win[:, 2 * rows_frame :]
    from_above = passed_along(lower_part.astype(jnp.bfloat16), "tile", -1).astype(lower_part.dtype)
    from_below = passed_along(upper_part.astype(jnp.bfloat16), "tile", 1).astype(upper_part.dtype)
    summed = middle + from_above + from_below
    key_out = summed[0].astype(jnp.bfloat16)
    value_out = summed[1].astype(jnp.bfloat16)
    attn_out, grad_query, grad_key, grad_value = (
        lax.all_to_all(out_rows, "head", split_axis=0, concat_axis=1, tiled=True),
        lax.all_to_all(dq_rows, "head", split_axis=0, concat_axis=1, tiled=True),
        lax.all_to_all(key_out, "head", split_axis=0, concat_axis=1, tiled=True),
        lax.all_to_all(value_out, "head", split_axis=0, concat_axis=1, tiled=True),
    )
    return (attn_out, grad_query, grad_key, grad_value)


def solution(mesh):
    in_specs = (
        P(("tile", "head"), None),
        P(("tile", "head"), None),
        P(("tile", "head"), None),
        P(("tile", "head"), None),
        P(),
        P(),
    )
    out_specs = (
        P(("tile", "head"), None),
        P(("tile", "head"), None),
        P(("tile", "head"), None),
        P(("tile", "head"), None),
    )
    return jax.shard_map(local, mesh=mesh, in_specs=in_specs, out_specs=out_specs, check_vma=False)
```

```python
import jax
import jax.numpy as jnp
from jax import lax
from jax.sharding import PartitionSpec as P
from jax.experimental import pallas as pl
from jax.experimental.pallas import tpu as pltpu

HD = 128


NEG = -1e30


def with_halo(array, sides, width):
    for axis, dim in sides:
        size, length = (lax.axis_size(axis), array.shape[dim])
        up = [(i, (i + 1) % size) for i in range(size - 1)]
        down = [(j, i) for i, j in up]
        last = lax.slice_in_dim(array, length - width, length, axis=dim)
        initial = lax.slice_in_dim(array, 0, width, axis=dim)
        before = lax.ppermute(last, axis, up)
        after = lax.ppermute(initial, axis, down)
        array = jnp.concatenate([before, array, after], axis=dim)
    return array


def passed_along(value, axis, steps):
    count = lax.axis_size(axis)
    initial, last = (max(0, -steps), min(count, count - steps))
    return lax.ppermute(value, axis, [(source, source + steps) for source in range(initial, last)])


def window_lists(block_mask, tile_order, frame_idx, frames, per_frame):
    tile_count = per_frame * frames
    query_clip = lax.dynamic_slice_in_dim(tile_order, frame_idx * per_frame, per_frame)
    cand_slot = (frame_idx - 1) * per_frame + jnp.arange(3 * per_frame, dtype=jnp.int32)
    valid_slot = ((cand_slot >= 0) & (cand_slot < tile_count)).astype(jnp.int32)
    cand_clip = jnp.take(tile_order, jnp.clip(cand_slot, 0, tile_count - 1))
    forward_active = block_mask[query_clip[:, None], cand_clip[None, :]] * valid_slot[None, :]
    backward_active = block_mask[cand_clip[:, None], query_clip[None, :]] * valid_slot[:, None]
    return (forward_active, backward_active)


def compact_slots(forward_active, max_keys):
    slot_key = jnp.argsort(1 - forward_active, axis=1, stable=True)[:, :max_keys]
    live_slot = jnp.take_along_axis(forward_active, slot_key, axis=1) > 0
    return (slot_key, live_slot)


def attn_kernel(slot_ref, live_ref, q_ref, g_ref, k_ref, v_ref, o_ref, dq_ref, dk_ref, dv_ref, kg_scr, vg_scr):
    tile_rows = HD
    query_tiles, max_keys = slot_ref.shape
    scaling = HD ** (-0.5)
    dk_ref[...] = jnp.zeros(dk_ref.shape, dk_ref.dtype)
    dv_ref[...] = jnp.zeros(dv_ref.shape, dv_ref.dtype)
    nt = (((1,), (1,)), ((), ()))
    tn = (((0,), (0,)), ((), ()))
    lane_slot = lax.broadcasted_iota(jnp.int32, (1, max_keys * tile_rows), 1) // tile_rows

    def key_rows(p, s):
        return pl.ds(pl.multiple_of(slot_ref[p, s] * tile_rows, tile_rows), tile_rows)

    def body(p, carry):
        rows = pl.ds(pl.multiple_of(p * tile_rows, tile_rows), tile_rows)
        live_lane = jnp.zeros((1, max_keys * tile_rows), jnp.int32)
        for s in range(max_keys):
            krows = key_rows(p, s)
            kg_scr[s * tile_rows : (s + 1) * tile_rows, :] = k_ref[krows, :]
            vg_scr[s * tile_rows : (s + 1) * tile_rows, :] = v_ref[krows, :]
            live_lane = jnp.where(lane_slot == s, live_ref[p, s], live_lane)
        q = q_ref[rows, :]
        g = g_ref[rows, :]
        kg = kg_scr[...]
        vg = vg_scr[...]
        sc = lax.dot_general(q, kg, nt, preferred_element_type=jnp.float32) * scaling
        sc = jnp.where(live_lane > 0, sc, NEG)
        top = jnp.max(sc, axis=1, keepdims=True)
        log_total = top + jnp.log(jnp.sum(jnp.exp(sc - top), axis=1, keepdims=True))
        prob = jnp.exp(sc - log_total)
        prob_bf = prob.astype(jnp.bfloat16)
        out = jnp.dot(prob_bf, vg, preferred_element_type=jnp.float32).astype(jnp.bfloat16)
        o_ref[rows, :] = out
        delta = jnp.sum(g.astype(jnp.float32) * out.astype(jnp.float32), axis=1, keepdims=True)
        dprob = lax.dot_general(g, vg, nt, preferred_element_type=jnp.float32)
        dscore = (prob * (dprob - delta)).astype(jnp.bfloat16)
        dq = jnp.dot(dscore, kg, preferred_element_type=jnp.float32) * scaling
        dq_ref[rows, :] = dq.astype(dq_ref.dtype)
        dk_g = lax.dot_general(dscore, q, tn, preferred_element_type=jnp.float32) * scaling
        dv_g = lax.dot_general(prob_bf, g, tn, preferred_element_type=jnp.float32)
        for s in range(max_keys):
            krows = key_rows(p, s)
            dk_ref[krows, :] += dk_g[s * tile_rows : (s + 1) * tile_rows, :]
            dv_ref[krows, :] += dv_g[s * tile_rows : (s + 1) * tile_rows, :]
        return carry

    lax.fori_loop(0, query_tiles, body, 0)


def attention_heads(q_loc, g_loc, k_win, v_win, slot_key, live_slot):
    rows_frame, width = q_loc.shape
    window_rows = k_win.shape[0]
    query_tiles, max_keys = slot_key.shape
    head_count = width // HD
    row_spec = pl.BlockSpec((rows_frame, HD), lambda h, *_: (0, h))
    win_spec = pl.BlockSpec((window_rows, HD), lambda h, *_: (0, h))
    flops = 12 * query_tiles * max_keys * HD * HD * HD * head_count
    grid_spec = pltpu.PrefetchScalarGridSpec(
        num_scalar_prefetch=2,
        grid=(head_count,),
        in_specs=[row_spec, row_spec, win_spec, win_spec],
        out_specs=[row_spec, row_spec, win_spec, win_spec],
        scratch_shapes=[
            pltpu.VMEM((max_keys * HD, HD), jnp.bfloat16),
            pltpu.VMEM((max_keys * HD, HD), jnp.bfloat16),
        ],
    )
    return pl.pallas_call(
        attn_kernel,
        grid_spec=grid_spec,
        out_shape=[
            jax.ShapeDtypeStruct((rows_frame, width), jnp.bfloat16),
            jax.ShapeDtypeStruct((rows_frame, width), jnp.bfloat16),
            jax.ShapeDtypeStruct((window_rows, width), jnp.float32),
            jax.ShapeDtypeStruct((window_rows, width), jnp.float32),
        ],
        cost_estimate=pl.CostEstimate(
            flops=flops,
            transcendentals=2 * query_tiles * max_keys * HD * HD * head_count,
            bytes_accessed=2 * (4 * rows_frame + 2 * window_rows) * width + 8 * window_rows * width,
        ),
    )(slot_key, live_slot.astype(jnp.int32), q_loc, g_loc, k_win, v_win)


def local(query, key, value, grad_out, block_mask, tile_order):
    per_frame = lax.axis_size("head")
    frames = lax.axis_size("tile")
    frame_idx = lax.axis_index("tile")
    max_keys = 3 * min(3, per_frame // 2)
    tile_rows = query.shape[0]
    q_loc, k_loc, v_loc, g_loc = (
        lax.all_to_all(query, "head", split_axis=1, concat_axis=0, tiled=True),
        lax.all_to_all(key, "head", split_axis=1, concat_axis=0, tiled=True),
        lax.all_to_all(value, "head", split_axis=1, concat_axis=0, tiled=True),
        lax.all_to_all(grad_out, "head", split_axis=1, concat_axis=0, tiled=True),
    )
    width_dev = q_loc.shape[1]
    head_count = width_dev // HD
    rows_frame = per_frame * tile_rows
    scaling = HD ** (-0.5)
    kv_rims = with_halo(jnp.stack([k_loc, v_loc]), (("tile", 1),), rows_frame)
    forward_active, backward_active = window_lists(
        block_mask, tile_order, frame_idx, frames, per_frame
    )
    slot_key, live_slot = compact_slots(forward_active, max_keys)
    out_rows, dq_rows, key_grad_win, value_grad_win = attention_heads(
        q_loc, g_loc, kv_rims[0], kv_rims[1], slot_key, live_slot
    )
    grads_win = jnp.stack([key_grad_win, value_grad_win])
    middle = grads_win[:, rows_frame : 2 * rows_frame]
    lower_part = grads_win[:, :rows_frame]
    upper_part = grads_win[:, 2 * rows_frame :]
    from_above = passed_along(lower_part.astype(jnp.bfloat16), "tile", -1).astype(lower_part.dtype)
    from_below = passed_along(upper_part.astype(jnp.bfloat16), "tile", 1).astype(upper_part.dtype)
    summed = middle + from_above + from_below
    key_out = summed[0].astype(jnp.bfloat16)
    value_out = summed[1].astype(jnp.bfloat16)
    attn_out, grad_query, grad_key, grad_value = (
        lax.all_to_all(out_rows, "head", split_axis=0, concat_axis=1, tiled=True),
        lax.all_to_all(dq_rows, "head", split_axis=0, concat_axis=1, tiled=True),
        lax.all_to_all(key_out, "head", split_axis=0, concat_axis=1, tiled=True),
        lax.all_to_all(value_out, "head", split_axis=0, concat_axis=1, tiled=True),
    )
    return (attn_out, grad_query, grad_key, grad_value)


def solution(mesh):
    in_specs = (
        P(("tile", "head"), None),
        P(("tile", "head"), None),
        P(("tile", "head"), None),
        P(("tile", "head"), None),
        P(),
        P(),
    )
    out_specs = (
        P(("tile", "head"), None),
        P(("tile", "head"), None),
        P(("tile", "head"), None),
        P(("tile", "head"), None),
    )
    return jax.shard_map(local, mesh=mesh, in_specs=in_specs, out_specs=out_specs, check_vma=False)
```

```python
import jax
import jax.numpy as jnp
from jax import lax
from jax.sharding import PartitionSpec as P
from jax.experimental import pallas as pl
from jax.experimental.pallas import tpu as pltpu

HD = 128


NEG = -1e30


def with_halo(array, sides, width):
    for axis, dim in sides:
        size, length = (lax.axis_size(axis), array.shape[dim])
        up = [(i, (i + 1) % size) for i in range(size - 1)]
        down = [(j, i) for i, j in up]
        last = lax.slice_in_dim(array, length - width, length, axis=dim)
        initial = lax.slice_in_dim(array, 0, width, axis=dim)
        before = lax.ppermute(last, axis, up)
        after = lax.ppermute(initial, axis, down)
        array = jnp.concatenate([before, array, after], axis=dim)
    return array


def passed_along(value, axis, steps):
    count = lax.axis_size(axis)
    initial, last = (max(0, -steps), min(count, count - steps))
    return lax.ppermute(value, axis, [(source, source + steps) for source in range(initial, last)])


def window_lists(block_mask, tile_order, frame_idx, frames, per_frame):
    tile_count = per_frame * frames
    query_clip = lax.dynamic_slice_in_dim(tile_order, frame_idx * per_frame, per_frame)
    cand_slot = (frame_idx - 1) * per_frame + jnp.arange(3 * per_frame, dtype=jnp.int32)
    valid_slot = ((cand_slot >= 0) & (cand_slot < tile_count)).astype(jnp.int32)
    cand_clip = jnp.take(tile_order, jnp.clip(cand_slot, 0, tile_count - 1))
    forward_active = block_mask[query_clip[:, None], cand_clip[None, :]] * valid_slot[None, :]
    backward_active = block_mask[cand_clip[:, None], query_clip[None, :]] * valid_slot[:, None]
    return (forward_active, backward_active)


def compact_slots(forward_active, max_keys):
    slot_key = jnp.argsort(1 - forward_active, axis=1, stable=True)[:, :max_keys]
    live_slot = jnp.take_along_axis(forward_active, slot_key, axis=1) > 0
    return (slot_key, live_slot)


def attn_kernel(slot_ref, live_ref, q_ref, g_ref, k_ref, v_ref, o_ref, dq_ref, dk_ref, dv_ref, kg_scr, vg_scr):
    tile_rows = HD
    query_tiles, max_keys = slot_ref.shape
    scaling = HD ** (-0.5)
    dk_ref[...] = jnp.zeros(dk_ref.shape, dk_ref.dtype)
    dv_ref[...] = jnp.zeros(dv_ref.shape, dv_ref.dtype)
    nt = (((1,), (1,)), ((), ()))
    tn = (((0,), (0,)), ((), ()))
    lane_slot = lax.broadcasted_iota(jnp.int32, (1, max_keys * tile_rows), 1) // tile_rows

    def key_rows(p, s):
        return pl.ds(pl.multiple_of(slot_ref[p, s] * tile_rows, tile_rows), tile_rows)

    def body(p, carry):
        rows = pl.ds(pl.multiple_of(p * tile_rows, tile_rows), tile_rows)
        live_lane = jnp.zeros((1, max_keys * tile_rows), jnp.int32)
        for s in range(max_keys):
            krows = key_rows(p, s)
            kg_scr[s * tile_rows : (s + 1) * tile_rows, :] = k_ref[krows, :]
            vg_scr[s * tile_rows : (s + 1) * tile_rows, :] = v_ref[krows, :]
            live_lane = jnp.where(lane_slot == s, live_ref[p, s], live_lane)
        q = q_ref[rows, :]
        g = g_ref[rows, :]
        kg = kg_scr[...]
        vg = vg_scr[...]
        sc = lax.dot_general(q, kg, nt, preferred_element_type=jnp.float32) * scaling
        sc = jnp.where(live_lane > 0, sc, NEG)
        top = jnp.max(sc, axis=1, keepdims=True)
        log_total = top + jnp.log(jnp.sum(jnp.exp(sc - top), axis=1, keepdims=True))
        prob = jnp.exp(sc - log_total)
        prob_bf = prob.astype(jnp.bfloat16)
        out = jnp.dot(prob_bf, vg, preferred_element_type=jnp.float32).astype(jnp.bfloat16)
        o_ref[rows, :] = out
        delta = jnp.sum(g.astype(jnp.float32) * out.astype(jnp.float32), axis=1, keepdims=True)
        dprob = lax.dot_general(g, vg, nt, preferred_element_type=jnp.float32)
        dscore = (prob * (dprob - delta)).astype(jnp.bfloat16)
        dq = jnp.dot(dscore, kg, preferred_element_type=jnp.float32) * scaling
        dq_ref[rows, :] = dq.astype(dq_ref.dtype)
        dk_g = lax.dot_general(dscore, q, tn, preferred_element_type=jnp.float32) * scaling
        dv_g = lax.dot_general(prob_bf, g, tn, preferred_element_type=jnp.float32)
        for s in range(max_keys):
            krows = key_rows(p, s)
            dk_ref[krows, :] += dk_g[s * tile_rows : (s + 1) * tile_rows, :]
            dv_ref[krows, :] += dv_g[s * tile_rows : (s + 1) * tile_rows, :]
        return carry

    lax.fori_loop(0, query_tiles, body, 0)


def attention_heads(q_loc, g_loc, k_win, v_win, slot_key, live_slot):
    rows_frame, width = q_loc.shape
    window_rows = k_win.shape[0]
    query_tiles, max_keys = slot_key.shape
    head_count = width // HD
    row_spec = pl.BlockSpec((rows_frame, HD), lambda h, *_: (0, h))
    win_spec = pl.BlockSpec((window_rows, HD), lambda h, *_: (0, h))
    flops = 12 * query_tiles * max_keys * HD * HD * HD * head_count
    grid_spec = pltpu.PrefetchScalarGridSpec(
        num_scalar_prefetch=2,
        grid=(head_count,),
        in_specs=[row_spec, row_spec, win_spec, win_spec],
        out_specs=[row_spec, row_spec, win_spec, win_spec],
        scratch_shapes=[
            pltpu.VMEM((max_keys * HD, HD), jnp.bfloat16),
            pltpu.VMEM((max_keys * HD, HD), jnp.bfloat16),
        ],
    )
    return pl.pallas_call(
        attn_kernel,
        grid_spec=grid_spec,
        out_shape=[
            jax.ShapeDtypeStruct((rows_frame, width), jnp.bfloat16),
            jax.ShapeDtypeStruct((rows_frame, width), jnp.bfloat16),
            jax.ShapeDtypeStruct((window_rows, width), jnp.float32),
            jax.ShapeDtypeStruct((window_rows, width), jnp.float32),
        ],
        cost_estimate=pl.CostEstimate(
            flops=flops,
            transcendentals=2 * query_tiles * max_keys * HD * HD * head_count,
            bytes_accessed=2 * (4 * rows_frame + 2 * window_rows) * width + 8 * window_rows * width,
        ),
    )(slot_key, live_slot.astype(jnp.int32), q_loc, g_loc, k_win, v_win)


def head_columns(array, head, groups):
    rows, width = array.shape
    per_group = width // (groups * HD)
    block = array.reshape(rows, groups, per_group, HD)[:, :, head, :]
    return jnp.transpose(block, (1, 0, 2))


def gather_heads(arrays, head, groups):
    stacked = jnp.stack([head_columns(x, head, groups) for x in arrays])
    moved = lax.all_to_all(stacked, "head", split_axis=1, concat_axis=1, tiled=True)
    return moved.reshape(len(arrays), groups * stacked.shape[2], HD)


def scatter_heads(arrays, groups):
    stacked = jnp.stack(arrays)
    count, rows_frame, _ = stacked.shape
    stacked = stacked.reshape(count, groups, rows_frame // groups, HD)
    return lax.all_to_all(stacked, "head", split_axis=1, concat_axis=1, tiled=True)


def local(query, key, value, grad_out, block_mask, tile_order):
    per_frame = lax.axis_size("head")
    frames = lax.axis_size("tile")
    frame_idx = lax.axis_index("tile")
    max_keys = 3 * min(3, per_frame // 2)
    tile_rows, width = query.shape
    head_count = width // (per_frame * HD)
    rows_frame = per_frame * tile_rows
    forward_active, _ = window_lists(block_mask, tile_order, frame_idx, frames, per_frame)
    slot_key, live_slot = compact_slots(forward_active, max_keys)
    fwd_parts, grad_parts = [], []
    for head in range(head_count):
        kv = gather_heads([key, value], head, per_frame)
        qg = gather_heads([query, grad_out], head, per_frame)
        kv_rims = with_halo(kv, (("tile", 1),), rows_frame)
        out_h, dq_h, dk_win, dv_win = attention_heads(
            qg[0], qg[1], kv_rims[0], kv_rims[1], slot_key, live_slot
        )
        fwd_parts.append(scatter_heads([out_h, dq_h], per_frame))
        grads_win = jnp.stack([dk_win, dv_win])
        middle = grads_win[:, rows_frame : 2 * rows_frame]
        lower_part = grads_win[:, :rows_frame]
        upper_part = grads_win[:, 2 * rows_frame :]
        from_above = passed_along(lower_part.astype(jnp.bfloat16), "tile", -1).astype(jnp.float32)
        from_below = passed_along(upper_part.astype(jnp.bfloat16), "tile", 1).astype(jnp.float32)
        summed = (middle + from_above + from_below).astype(jnp.bfloat16)
        grad_parts.append(scatter_heads([summed[0], summed[1]], per_frame))

    def assemble(parts):
        stacked = jnp.stack(parts, axis=2)
        count = stacked.shape[0]
        return jnp.transpose(stacked, (0, 3, 1, 2, 4)).reshape(count, tile_rows, width)

    fwd = assemble(fwd_parts)
    grads = assemble(grad_parts)
    return (fwd[0], fwd[1], grads[0], grads[1])


def solution(mesh):
    in_specs = (
        P(("tile", "head"), None),
        P(("tile", "head"), None),
        P(("tile", "head"), None),
        P(("tile", "head"), None),
        P(),
        P(),
    )
    out_specs = (
        P(("tile", "head"), None),
        P(("tile", "head"), None),
        P(("tile", "head"), None),
        P(("tile", "head"), None),
    )
    return jax.shard_map(local, mesh=mesh, in_specs=in_specs, out_specs=out_specs, check_vma=False)
```

```python
import jax
import jax.numpy as jnp
from jax import lax
from jax.sharding import PartitionSpec as P
from jax.experimental import pallas as pl
from jax.experimental.pallas import tpu as pltpu

HD = 128


NEG = -1e30


def with_halo(array, sides, width):
    for axis, dim in sides:
        size, length = (lax.axis_size(axis), array.shape[dim])
        up = [(i, (i + 1) % size) for i in range(size - 1)]
        down = [(j, i) for i, j in up]
        last = lax.slice_in_dim(array, length - width, length, axis=dim)
        initial = lax.slice_in_dim(array, 0, width, axis=dim)
        before = lax.ppermute(last, axis, up)
        after = lax.ppermute(initial, axis, down)
        array = jnp.concatenate([before, array, after], axis=dim)
    return array


def passed_along(value, axis, steps):
    count = lax.axis_size(axis)
    initial, last = (max(0, -steps), min(count, count - steps))
    return lax.ppermute(value, axis, [(source, source + steps) for source in range(initial, last)])


def window_lists(block_mask, tile_order, frame_idx, frames, per_frame):
    tile_count = per_frame * frames
    query_clip = lax.dynamic_slice_in_dim(tile_order, frame_idx * per_frame, per_frame)
    cand_slot = (frame_idx - 1) * per_frame + jnp.arange(3 * per_frame, dtype=jnp.int32)
    valid_slot = ((cand_slot >= 0) & (cand_slot < tile_count)).astype(jnp.int32)
    cand_clip = jnp.take(tile_order, jnp.clip(cand_slot, 0, tile_count - 1))
    forward_active = block_mask[query_clip[:, None], cand_clip[None, :]] * valid_slot[None, :]
    backward_active = block_mask[cand_clip[:, None], query_clip[None, :]] * valid_slot[:, None]
    return (forward_active, backward_active)


def compact_slots(forward_active, max_keys):
    slot_key = jnp.argsort(1 - forward_active, axis=1, stable=True)[:, :max_keys]
    live_slot = jnp.take_along_axis(forward_active, slot_key, axis=1) > 0
    return (slot_key, live_slot)


def attn_kernel(
    slot_ref, live_ref, qg_ref, prev_ref, own_ref, next_ref,
    og_ref, gown_ref, gprev_ref, gnext_ref, kg_scr, vg_scr, acc_scr,
):
    tile_rows = HD
    query_tiles, max_keys = slot_ref.shape
    scaling = HD ** (-0.5)
    window = (prev_ref, own_ref, next_ref)
    acc_scr[...] = jnp.zeros(acc_scr.shape, acc_scr.dtype)
    nt = (((1,), (1,)), ((), ()))
    tn = (((0,), (0,)), ((), ()))
    lane_slot = lax.broadcasted_iota(jnp.int32, (1, max_keys * tile_rows), 1) // tile_rows

    def acc_rows(p, s):
        return pl.ds(pl.multiple_of(slot_ref[p, s] * tile_rows, tile_rows), tile_rows)

    def body(p, carry):
        rows = pl.ds(pl.multiple_of(p * tile_rows, tile_rows), tile_rows)
        live_lane = jnp.zeros((1, max_keys * tile_rows), jnp.int32)
        for s in range(max_keys):
            slot = slot_ref[p, s]
            side = slot // query_tiles
            src = pl.ds(pl.multiple_of((slot % query_tiles) * tile_rows, tile_rows), tile_rows)
            dst = slice(s * tile_rows, (s + 1) * tile_rows)
            for w in range(3):

                @pl.when(side == w)
                def _():
                    kg_scr[dst, :] = window[w][0, src, :]
                    vg_scr[dst, :] = window[w][1, src, :]

            live_lane = jnp.where(lane_slot == s, live_ref[p, s], live_lane)
        q = qg_ref[0, rows, :]
        g = qg_ref[1, rows, :]
        kg = kg_scr[...]
        vg = vg_scr[...]
        sc = lax.dot_general(q, kg, nt, preferred_element_type=jnp.float32) * scaling
        sc = jnp.where(live_lane > 0, sc, NEG)
        top = jnp.max(sc, axis=1, keepdims=True)
        log_total = top + jnp.log(jnp.sum(jnp.exp(sc - top), axis=1, keepdims=True))
        prob = jnp.exp(sc - log_total)
        prob_bf = prob.astype(jnp.bfloat16)
        out = jnp.dot(prob_bf, vg, preferred_element_type=jnp.float32).astype(jnp.bfloat16)
        og_ref[0, rows, :] = out
        delta = jnp.sum(g.astype(jnp.float32) * out.astype(jnp.float32), axis=1, keepdims=True)
        dprob = lax.dot_general(g, vg, nt, preferred_element_type=jnp.float32)
        dscore = (prob * (dprob - delta)).astype(jnp.bfloat16)
        dq = jnp.dot(dscore, kg, preferred_element_type=jnp.float32) * scaling
        og_ref[1, rows, :] = dq.astype(og_ref.dtype)
        dk_g = lax.dot_general(dscore, q, tn, preferred_element_type=jnp.float32) * scaling
        dv_g = lax.dot_general(prob_bf, g, tn, preferred_element_type=jnp.float32)
        for s in range(max_keys):
            arows = acc_rows(p, s)
            acc_scr[0, arows, :] += dk_g[s * tile_rows : (s + 1) * tile_rows, :]
            acc_scr[1, arows, :] += dv_g[s * tile_rows : (s + 1) * tile_rows, :]
        return carry

    lax.fori_loop(0, query_tiles, body, 0)
    rows_frame = query_tiles * tile_rows
    gprev_ref[...] = acc_scr[:, :rows_frame, :].astype(gprev_ref.dtype)
    gown_ref[...] = acc_scr[:, rows_frame : 2 * rows_frame, :]
    gnext_ref[...] = acc_scr[:, 2 * rows_frame :, :].astype(gnext_ref.dtype)


def attention_heads(qg, kv_prev, kv_own, kv_next, slot_key, live_slot):
    _, rows_frame, width = qg.shape
    query_tiles, max_keys = slot_key.shape
    head_count = width // HD
    spec = pl.BlockSpec((2, rows_frame, HD), lambda h, *_: (0, 0, h))
    flops = 12 * query_tiles * max_keys * HD * HD * HD * head_count
    grid_spec = pltpu.PrefetchScalarGridSpec(
        num_scalar_prefetch=2,
        grid=(head_count,),
        in_specs=[spec, spec, spec, spec],
        out_specs=[spec, spec, spec, spec],
        scratch_shapes=[
            pltpu.VMEM((max_keys * HD, HD), jnp.bfloat16),
            pltpu.VMEM((max_keys * HD, HD), jnp.bfloat16),
            pltpu.VMEM((2, 3 * rows_frame, HD), jnp.float32),
        ],
    )
    block = (2, rows_frame, width)
    return pl.pallas_call(
        attn_kernel,
        grid_spec=grid_spec,
        out_shape=[
            jax.ShapeDtypeStruct(block, jnp.bfloat16),
            jax.ShapeDtypeStruct(block, jnp.float32),
            jax.ShapeDtypeStruct(block, jnp.bfloat16),
            jax.ShapeDtypeStruct(block, jnp.bfloat16),
        ],
        cost_estimate=pl.CostEstimate(
            flops=flops,
            transcendentals=query_tiles * max_keys * HD * HD * head_count,
            bytes_accessed=2 * rows_frame * width * 2 * 8,
        ),
    )(slot_key, live_slot.astype(jnp.int32), qg, kv_prev, kv_own, kv_next)


def to_heads(arrays):
    return lax.all_to_all(jnp.stack(arrays), "head", split_axis=2, concat_axis=1, tiled=True)


def to_tokens(stacked):
    return lax.all_to_all(stacked, "head", split_axis=1, concat_axis=2, tiled=True)


def local(query, key, value, grad_out, block_mask, tile_order):
    per_frame = lax.axis_size("head")
    frames = lax.axis_size("tile")
    frame_idx = lax.axis_index("tile")
    max_keys = 3 * min(3, per_frame // 2)
    forward_active, _ = window_lists(block_mask, tile_order, frame_idx, frames, per_frame)
    slot_key, live_slot = compact_slots(forward_active, max_keys)
    kv = to_heads([key, value])
    kv_prev = passed_along(kv, "tile", 1)
    kv_next = passed_along(kv, "tile", -1)
    qg = to_heads([query, grad_out])
    og, grad_own, grad_prev, grad_next = attention_heads(
        qg, kv_prev, kv, kv_next, slot_key, live_slot
    )
    og_tok = to_tokens(og)
    from_above = passed_along(grad_prev, "tile", -1).astype(jnp.float32)
    from_below = passed_along(grad_next, "tile", 1).astype(jnp.float32)
    summed = (grad_own + from_above + from_below).astype(jnp.bfloat16)
    grads_tok = to_tokens(summed)
    return (og_tok[0], og_tok[1], grads_tok[0], grads_tok[1])


def solution(mesh):
    in_specs = (
        P(("tile", "head"), None),
        P(("tile", "head"), None),
        P(("tile", "head"), None),
        P(("tile", "head"), None),
        P(),
        P(),
    )
    out_specs = (
        P(("tile", "head"), None),
        P(("tile", "head"), None),
        P(("tile", "head"), None),
        P(("tile", "head"), None),
    )
    return jax.shard_map(local, mesh=mesh, in_specs=in_specs, out_specs=out_specs, check_vma=False)
```

```python
import jax
import jax.numpy as jnp
from jax import lax
from jax.sharding import PartitionSpec as P
from jax.experimental import pallas as pl
from jax.experimental.pallas import tpu as pltpu

HD = 128


NEG = -1e30


def with_halo(array, sides, width):
    for axis, dim in sides:
        size, length = (lax.axis_size(axis), array.shape[dim])
        up = [(i, (i + 1) % size) for i in range(size - 1)]
        down = [(j, i) for i, j in up]
        last = lax.slice_in_dim(array, length - width, length, axis=dim)
        initial = lax.slice_in_dim(array, 0, width, axis=dim)
        before = lax.ppermute(last, axis, up)
        after = lax.ppermute(initial, axis, down)
        array = jnp.concatenate([before, array, after], axis=dim)
    return array


def passed_along(value, axis, steps):
    count = lax.axis_size(axis)
    initial, last = (max(0, -steps), min(count, count - steps))
    return lax.ppermute(value, axis, [(source, source + steps) for source in range(initial, last)])


def window_lists(block_mask, tile_order, frame_idx, frames, per_frame):
    tile_count = per_frame * frames
    query_clip = lax.dynamic_slice_in_dim(tile_order, frame_idx * per_frame, per_frame)
    cand_slot = (frame_idx - 1) * per_frame + jnp.arange(3 * per_frame, dtype=jnp.int32)
    valid_slot = ((cand_slot >= 0) & (cand_slot < tile_count)).astype(jnp.int32)
    cand_clip = jnp.take(tile_order, jnp.clip(cand_slot, 0, tile_count - 1))
    forward_active = block_mask[query_clip[:, None], cand_clip[None, :]] * valid_slot[None, :]
    backward_active = block_mask[cand_clip[:, None], query_clip[None, :]] * valid_slot[:, None]
    return (forward_active, backward_active)


def compact_slots(forward_active, max_keys):
    slot_key = jnp.argsort(1 - forward_active, axis=1, stable=True)[:, :max_keys]
    live_slot = jnp.take_along_axis(forward_active, slot_key, axis=1) > 0
    return (slot_key, live_slot)


def attn_kernel(
    slot_ref, live_ref, qg_ref, prev_ref, own_ref, next_ref,
    og_ref, gown_ref, gprev_ref, gnext_ref, kg_scr, vg_scr, acc_scr,
):
    tile_rows = HD
    query_tiles, max_keys = slot_ref.shape
    scaling = HD ** (-0.5)
    window = (prev_ref, own_ref, next_ref)
    acc_scr[...] = jnp.zeros(acc_scr.shape, acc_scr.dtype)
    nt = (((1,), (1,)), ((), ()))
    tn = (((0,), (0,)), ((), ()))
    lane_slot = lax.broadcasted_iota(jnp.int32, (1, max_keys * tile_rows), 1) // tile_rows

    def body(p, carry):
        live_lane = jnp.zeros((1, max_keys * tile_rows), jnp.int32)
        for s in range(max_keys):
            slot = slot_ref[p, s]
            side = slot // query_tiles
            tile = slot % query_tiles
            dst = slice(s * tile_rows, (s + 1) * tile_rows)
            for w in range(3):

                @pl.when(side == w)
                def _():
                    kg_scr[dst, :] = window[w][tile, 0]
                    vg_scr[dst, :] = window[w][tile, 1]

            live_lane = jnp.where(lane_slot == s, live_ref[p, s], live_lane)
        q = qg_ref[p, 0]
        g = qg_ref[p, 1]
        kg = kg_scr[...]
        vg = vg_scr[...]
        sc = lax.dot_general(q, kg, nt, preferred_element_type=jnp.float32) * scaling
        sc = jnp.where(live_lane > 0, sc, NEG)
        top = jnp.max(sc, axis=1, keepdims=True)
        expd = jnp.exp(sc - top)
        prob = expd * (1.0 / jnp.sum(expd, axis=1, keepdims=True))
        prob_bf = prob.astype(jnp.bfloat16)
        out = jnp.dot(prob_bf, vg, preferred_element_type=jnp.float32).astype(jnp.bfloat16)
        og_ref[p, 0] = out
        delta = jnp.sum(g.astype(jnp.float32) * out.astype(jnp.float32), axis=1, keepdims=True)
        dprob = lax.dot_general(g, vg, nt, preferred_element_type=jnp.float32)
        dscore = (prob * (dprob - delta)).astype(jnp.bfloat16)
        dq = jnp.dot(dscore, kg, preferred_element_type=jnp.float32) * scaling
        og_ref[p, 1] = dq.astype(og_ref.dtype)
        dk_g = lax.dot_general(dscore, q, tn, preferred_element_type=jnp.float32) * scaling
        dv_g = lax.dot_general(prob_bf, g, tn, preferred_element_type=jnp.float32)
        for s in range(max_keys):
            slot = slot_ref[p, s]
            acc_scr[slot, 0] += dk_g[s * tile_rows : (s + 1) * tile_rows, :]
            acc_scr[slot, 1] += dv_g[s * tile_rows : (s + 1) * tile_rows, :]
        return carry

    lax.fori_loop(0, query_tiles, body, 0)
    gprev_ref[...] = acc_scr[:query_tiles].astype(gprev_ref.dtype)
    gown_ref[...] = acc_scr[query_tiles : 2 * query_tiles]
    gnext_ref[...] = acc_scr[2 * query_tiles :].astype(gnext_ref.dtype)


def attention_heads(qg, kv_prev, kv_own, kv_next, slot_key, live_slot):
    query_tiles, count, tile_rows, width = qg.shape
    max_keys = slot_key.shape[1]
    head_count = width // HD
    spec = pl.BlockSpec((query_tiles, count, tile_rows, HD), lambda h, *_: (0, 0, 0, h))
    flops = 12 * query_tiles * max_keys * tile_rows * tile_rows * HD * head_count
    grid_spec = pltpu.PrefetchScalarGridSpec(
        num_scalar_prefetch=2,
        grid=(head_count,),
        in_specs=[spec, spec, spec, spec],
        out_specs=[spec, spec, spec, spec],
        scratch_shapes=[
            pltpu.VMEM((max_keys * tile_rows, HD), jnp.bfloat16),
            pltpu.VMEM((max_keys * tile_rows, HD), jnp.bfloat16),
            pltpu.VMEM((3 * query_tiles, count, tile_rows, HD), jnp.float32),
        ],
    )
    block = qg.shape
    return pl.pallas_call(
        attn_kernel,
        grid_spec=grid_spec,
        out_shape=[
            jax.ShapeDtypeStruct(block, jnp.bfloat16),
            jax.ShapeDtypeStruct(block, jnp.float32),
            jax.ShapeDtypeStruct(block, jnp.bfloat16),
            jax.ShapeDtypeStruct(block, jnp.bfloat16),
        ],
        cost_estimate=pl.CostEstimate(
            flops=flops,
            transcendentals=query_tiles * max_keys * tile_rows * tile_rows * head_count,
            bytes_accessed=query_tiles * count * tile_rows * width * 2 * 8,
        ),
    )(slot_key, live_slot.astype(jnp.int32), qg, kv_prev, kv_own, kv_next)


def split_kernel(*refs):
    count = len(refs) - 1
    for i in range(count):
        refs[-1][0, i] = refs[i][...]


def join_kernel(*refs):
    count = len(refs) - 1
    for i in range(count):
        refs[1 + i][...] = refs[0][0, i]


def split_columns(arrays, groups):
    rows, width = arrays[0].shape
    part = width // groups
    count = len(arrays)
    return pl.pallas_call(
        split_kernel,
        grid=(groups,),
        in_specs=[pl.BlockSpec((rows, part), lambda j: (0, j))] * count,
        out_specs=pl.BlockSpec((1, count, rows, part), lambda j: (j, 0, 0, 0)),
        out_shape=jax.ShapeDtypeStruct((groups, count, rows, part), arrays[0].dtype),
    )(*arrays)


def join_columns(stacked):
    groups, count, rows, part = stacked.shape
    return pl.pallas_call(
        join_kernel,
        grid=(groups,),
        in_specs=[pl.BlockSpec((1, count, rows, part), lambda j: (j, 0, 0, 0))],
        out_specs=[pl.BlockSpec((rows, part), lambda j: (0, j))] * count,
        out_shape=[jax.ShapeDtypeStruct((rows, groups * part), stacked.dtype)] * count,
    )(stacked)


def to_heads(arrays, groups):
    stacked = split_columns(arrays, groups)
    return lax.all_to_all(stacked, "head", split_axis=0, concat_axis=0, tiled=True)


def to_tokens(stacked):
    moved = lax.all_to_all(stacked, "head", split_axis=0, concat_axis=0, tiled=True)
    return join_columns(moved)


def local(query, key, value, grad_out, block_mask, tile_order):
    per_frame = lax.axis_size("head")
    frames = lax.axis_size("tile")
    frame_idx = lax.axis_index("tile")
    max_keys = 3 * min(3, per_frame // 2)
    forward_active, _ = window_lists(block_mask, tile_order, frame_idx, frames, per_frame)
    slot_key, live_slot = compact_slots(forward_active, max_keys)
    kv = to_heads([key, value], per_frame)
    kv_prev = passed_along(kv, "tile", 1)
    kv_next = passed_along(kv, "tile", -1)
    qg = to_heads([query, grad_out], per_frame)
    og, grad_own, grad_prev, grad_next = attention_heads(
        qg, kv_prev, kv, kv_next, slot_key, live_slot
    )
    attn_out, grad_query = to_tokens(og)
    from_above = passed_along(grad_prev, "tile", -1).astype(jnp.float32)
    from_below = passed_along(grad_next, "tile", 1).astype(jnp.float32)
    summed = (grad_own + from_above + from_below).astype(jnp.bfloat16)
    grad_key, grad_value = to_tokens(summed)
    return (attn_out, grad_query, grad_key, grad_value)


def solution(mesh):
    in_specs = (
        P(("tile", "head"), None),
        P(("tile", "head"), None),
        P(("tile", "head"), None),
        P(("tile", "head"), None),
        P(),
        P(),
    )
    out_specs = (
        P(("tile", "head"), None),
        P(("tile", "head"), None),
        P(("tile", "head"), None),
        P(("tile", "head"), None),
    )
    return jax.shard_map(local, mesh=mesh, in_specs=in_specs, out_specs=out_specs, check_vma=False)
```

```python
import jax
import jax.numpy as jnp
from jax import lax
from jax.sharding import PartitionSpec as P
from jax.experimental import pallas as pl
from jax.experimental.pallas import tpu as pltpu

HD = 128


NEG = -1e30


def with_halo(array, sides, width):
    for axis, dim in sides:
        size, length = (lax.axis_size(axis), array.shape[dim])
        up = [(i, (i + 1) % size) for i in range(size - 1)]
        down = [(j, i) for i, j in up]
        last = lax.slice_in_dim(array, length - width, length, axis=dim)
        initial = lax.slice_in_dim(array, 0, width, axis=dim)
        before = lax.ppermute(last, axis, up)
        after = lax.ppermute(initial, axis, down)
        array = jnp.concatenate([before, array, after], axis=dim)
    return array


def passed_along(value, axis, steps):
    count = lax.axis_size(axis)
    initial, last = (max(0, -steps), min(count, count - steps))
    return lax.ppermute(value, axis, [(source, source + steps) for source in range(initial, last)])


def window_lists(block_mask, tile_order, frame_idx, frames, per_frame):
    tile_count = per_frame * frames
    query_clip = lax.dynamic_slice_in_dim(tile_order, frame_idx * per_frame, per_frame)
    cand_slot = (frame_idx - 1) * per_frame + jnp.arange(3 * per_frame, dtype=jnp.int32)
    valid_slot = ((cand_slot >= 0) & (cand_slot < tile_count)).astype(jnp.int32)
    cand_clip = jnp.take(tile_order, jnp.clip(cand_slot, 0, tile_count - 1))
    forward_active = block_mask[query_clip[:, None], cand_clip[None, :]] * valid_slot[None, :]
    backward_active = block_mask[cand_clip[:, None], query_clip[None, :]] * valid_slot[:, None]
    return (forward_active, backward_active)


def compact_slots(forward_active, max_keys):
    slot_key = jnp.argsort(1 - forward_active, axis=1, stable=True)[:, :max_keys]
    live_slot = jnp.take_along_axis(forward_active, slot_key, axis=1) > 0
    return (slot_key, live_slot)


def attn_kernel(
    slot_ref, live_ref, qg_ref, prev_ref, own_ref, next_ref,
    og_ref, gown_ref, gprev_ref, gnext_ref, kg_scr, vg_scr, acc_scr,
):
    tile_rows = HD
    query_tiles, max_keys = slot_ref.shape
    scaling = HD ** (-0.5)
    window = (prev_ref, own_ref, next_ref)
    acc_scr[...] = jnp.zeros(acc_scr.shape, acc_scr.dtype)
    nt = (((1,), (1,)), ((), ()))
    tn = (((0,), (0,)), ((), ()))
    lane_slot = lax.broadcasted_iota(jnp.int32, (1, max_keys * tile_rows), 1) // tile_rows

    def body(p, carry):
        live_lane = jnp.zeros((1, max_keys * tile_rows), jnp.int32)
        for s in range(max_keys):
            slot = slot_ref[p, s]
            side = slot // query_tiles
            tile = slot % query_tiles
            dst = slice(s * tile_rows, (s + 1) * tile_rows)
            for w in range(3):

                @pl.when(side == w)
                def _():
                    kg_scr[dst, :] = window[w][tile, 0]
                    vg_scr[dst, :] = window[w][tile, 1]

            live_lane = jnp.where(lane_slot == s, live_ref[p, s], live_lane)
        q = qg_ref[p, 0]
        g = qg_ref[p, 1]
        kg = kg_scr[...]
        vg = vg_scr[...]
        sc = lax.dot_general(q, kg, nt, preferred_element_type=jnp.float32) * scaling
        sc = jnp.where(live_lane > 0, sc, NEG)
        top = jnp.max(sc, axis=1, keepdims=True)
        expd = jnp.exp(sc - top)
        prob = expd * (1.0 / jnp.sum(expd, axis=1, keepdims=True))
        prob_bf = prob.astype(jnp.bfloat16)
        out = jnp.dot(prob_bf, vg, preferred_element_type=jnp.float32).astype(jnp.bfloat16)
        og_ref[p, 0] = out
        delta = jnp.sum(g.astype(jnp.float32) * out.astype(jnp.float32), axis=1, keepdims=True)
        dprob = lax.dot_general(g, vg, nt, preferred_element_type=jnp.float32)
        dscore = (prob * (dprob - delta)).astype(jnp.bfloat16)
        dq = jnp.dot(dscore, kg, preferred_element_type=jnp.float32) * scaling
        og_ref[p, 1] = dq.astype(og_ref.dtype)
        dk_g = lax.dot_general(dscore, q, tn, preferred_element_type=jnp.float32) * scaling
        dv_g = lax.dot_general(prob_bf, g, tn, preferred_element_type=jnp.float32)
        for s in range(max_keys):
            slot = slot_ref[p, s]
            acc_scr[slot, 0] += dk_g[s * tile_rows : (s + 1) * tile_rows, :]
            acc_scr[slot, 1] += dv_g[s * tile_rows : (s + 1) * tile_rows, :]
        return carry

    lax.fori_loop(0, query_tiles, body, 0, unroll=2)
    gprev_ref[...] = acc_scr[:query_tiles].astype(gprev_ref.dtype)
    gown_ref[...] = acc_scr[query_tiles : 2 * query_tiles]
    gnext_ref[...] = acc_scr[2 * query_tiles :].astype(gnext_ref.dtype)


def attention_heads(qg, kv_prev, kv_own, kv_next, slot_key, live_slot):
    query_tiles, count, tile_rows, width = qg.shape
    max_keys = slot_key.shape[1]
    head_count = width // HD
    spec = pl.BlockSpec((query_tiles, count, tile_rows, HD), lambda h, *_: (0, 0, 0, h))
    flops = 12 * query_tiles * max_keys * tile_rows * tile_rows * HD * head_count
    grid_spec = pltpu.PrefetchScalarGridSpec(
        num_scalar_prefetch=2,
        grid=(head_count,),
        in_specs=[spec, spec, spec, spec],
        out_specs=[spec, spec, spec, spec],
        scratch_shapes=[
            pltpu.VMEM((max_keys * tile_rows, HD), jnp.bfloat16),
            pltpu.VMEM((max_keys * tile_rows, HD), jnp.bfloat16),
            pltpu.VMEM((3 * query_tiles, count, tile_rows, HD), jnp.float32),
        ],
    )
    block = qg.shape
    return pl.pallas_call(
        attn_kernel,
        grid_spec=grid_spec,
        out_shape=[
            jax.ShapeDtypeStruct(block, jnp.bfloat16),
            jax.ShapeDtypeStruct(block, jnp.float32),
            jax.ShapeDtypeStruct(block, jnp.bfloat16),
            jax.ShapeDtypeStruct(block, jnp.bfloat16),
        ],
        cost_estimate=pl.CostEstimate(
            flops=flops,
            transcendentals=query_tiles * max_keys * tile_rows * tile_rows * head_count,
            bytes_accessed=query_tiles * count * tile_rows * width * 2 * 8,
        ),
    )(slot_key, live_slot.astype(jnp.int32), qg, kv_prev, kv_own, kv_next)


def split_kernel(*refs):
    count = len(refs) - 1
    groups, _, _, part = refs[-1].shape
    for j in range(groups):
        for i in range(count):
            refs[-1][j, i] = refs[i][:, j * part : (j + 1) * part]


def join_kernel(*refs):
    groups, count, _, part = refs[0].shape
    for j in range(groups):
        for i in range(count):
            refs[1 + i][:, j * part : (j + 1) * part] = refs[0][j, i]


def split_columns(arrays, groups):
    rows, width = arrays[0].shape
    part = width // groups
    count = len(arrays)
    return pl.pallas_call(
        split_kernel,
        in_specs=[pl.BlockSpec(memory_space=pltpu.VMEM)] * count,
        out_specs=pl.BlockSpec(memory_space=pltpu.VMEM),
        out_shape=jax.ShapeDtypeStruct((groups, count, rows, part), arrays[0].dtype),
    )(*arrays)


def join_columns(stacked):
    groups, count, rows, part = stacked.shape
    return pl.pallas_call(
        join_kernel,
        in_specs=[pl.BlockSpec(memory_space=pltpu.VMEM)],
        out_specs=[pl.BlockSpec(memory_space=pltpu.VMEM)] * count,
        out_shape=[jax.ShapeDtypeStruct((rows, groups * part), stacked.dtype)] * count,
    )(stacked)


def to_heads(arrays, groups):
    stacked = split_columns(arrays, groups)
    return lax.all_to_all(stacked, "head", split_axis=0, concat_axis=0, tiled=True)


def to_tokens(stacked):
    moved = lax.all_to_all(stacked, "head", split_axis=0, concat_axis=0, tiled=True)
    return join_columns(moved)


def local(query, key, value, grad_out, block_mask, tile_order):
    per_frame = lax.axis_size("head")
    frames = lax.axis_size("tile")
    frame_idx = lax.axis_index("tile")
    max_keys = 3 * min(3, per_frame // 2)
    forward_active, _ = window_lists(block_mask, tile_order, frame_idx, frames, per_frame)
    slot_key, live_slot = compact_slots(forward_active, max_keys)
    kv = to_heads([key, value], per_frame)
    kv_prev = passed_along(kv, "tile", 1)
    kv_next = passed_along(kv, "tile", -1)
    qg = to_heads([query, grad_out], per_frame)
    og, grad_own, grad_prev, grad_next = attention_heads(
        qg, kv_prev, kv, kv_next, slot_key, live_slot
    )
    attn_out, grad_query = to_tokens(og)
    from_above = passed_along(grad_prev, "tile", -1).astype(jnp.float32)
    from_below = passed_along(grad_next, "tile", 1).astype(jnp.float32)
    summed = (grad_own + from_above + from_below).astype(jnp.bfloat16)
    grad_key, grad_value = to_tokens(summed)
    return (attn_out, grad_query, grad_key, grad_value)


def solution(mesh):
    in_specs = (
        P(("tile", "head"), None),
        P(("tile", "head"), None),
        P(("tile", "head"), None),
        P(("tile", "head"), None),
        P(),
        P(),
    )
    out_specs = (
        P(("tile", "head"), None),
        P(("tile", "head"), None),
        P(("tile", "head"), None),
        P(("tile", "head"), None),
    )
    return jax.shard_map(local, mesh=mesh, in_specs=in_specs, out_specs=out_specs, check_vma=False)
```

```python
import jax
import jax.numpy as jnp
from jax import lax
from jax.sharding import PartitionSpec as P
from jax.experimental import pallas as pl
from jax.experimental.pallas import tpu as pltpu

HD = 128


NEG = -1e30


def with_halo(array, sides, width):
    for axis, dim in sides:
        size, length = (lax.axis_size(axis), array.shape[dim])
        up = [(i, (i + 1) % size) for i in range(size - 1)]
        down = [(j, i) for i, j in up]
        last = lax.slice_in_dim(array, length - width, length, axis=dim)
        initial = lax.slice_in_dim(array, 0, width, axis=dim)
        before = lax.ppermute(last, axis, up)
        after = lax.ppermute(initial, axis, down)
        array = jnp.concatenate([before, array, after], axis=dim)
    return array


def passed_along(value, axis, steps):
    count = lax.axis_size(axis)
    initial, last = (max(0, -steps), min(count, count - steps))
    return lax.ppermute(value, axis, [(source, source + steps) for source in range(initial, last)])


def window_lists(block_mask, tile_order, frame_idx, frames, per_frame):
    tile_count = per_frame * frames
    query_clip = lax.dynamic_slice_in_dim(tile_order, frame_idx * per_frame, per_frame)
    cand_slot = (frame_idx - 1) * per_frame + jnp.arange(3 * per_frame, dtype=jnp.int32)
    valid_slot = ((cand_slot >= 0) & (cand_slot < tile_count)).astype(jnp.int32)
    cand_clip = jnp.take(tile_order, jnp.clip(cand_slot, 0, tile_count - 1))
    forward_active = block_mask[query_clip[:, None], cand_clip[None, :]] * valid_slot[None, :]
    backward_active = block_mask[cand_clip[:, None], query_clip[None, :]] * valid_slot[:, None]
    return (forward_active, backward_active)


def compact_slots(forward_active, max_keys):
    slot_key = jnp.argsort(1 - forward_active, axis=1, stable=True)[:, :max_keys]
    live_slot = jnp.take_along_axis(forward_active, slot_key, axis=1) > 0
    return (slot_key, live_slot)


def attn_kernel(
    slot_ref, live_ref, qg_ref, prev_ref, own_ref, next_ref,
    og_ref, gown_ref, gprev_ref, gnext_ref, kg_scr, vg_scr, acc_scr, e_scr, pbf_scr, ds_scr,
):
    tile_rows = HD
    query_tiles, max_keys = slot_ref.shape
    scaling = HD ** (-0.5)
    window = (prev_ref, own_ref, next_ref)
    acc_scr[...] = jnp.zeros(acc_scr.shape, acc_scr.dtype)
    nt = (((1,), (1,)), ((), ()))
    tn = (((0,), (0,)), ((), ()))

    def body(p, carry):
        for s in range(max_keys):
            slot = slot_ref[p, s]
            side = slot // query_tiles
            tile = slot % query_tiles
            dst = slice(s * tile_rows, (s + 1) * tile_rows)
            for w in range(3):

                @pl.when(side == w)
                def _():
                    kg_scr[dst, :] = window[w][tile, 0]
                    vg_scr[dst, :] = window[w][tile, 1]

        q = qg_ref[p, 0]
        g = qg_ref[p, 1]
        kg = kg_scr[...]
        vg = vg_scr[...]
        sc = lax.dot_general(q, kg, nt, preferred_element_type=jnp.float32)

        def masked(s):
            chunk = sc[:, s * tile_rows : (s + 1) * tile_rows] * scaling
            return jnp.where(live_ref[p, s] > 0, chunk, NEG)

        run_max = masked(0)
        for s in range(1, max_keys):
            run_max = jnp.maximum(run_max, masked(s))
        top = jnp.max(run_max, axis=1, keepdims=True)
        run_sum = jnp.zeros((tile_rows, tile_rows), jnp.float32)
        for s in range(max_keys):
            expd = jnp.exp(masked(s) - top)
            e_scr[:, s * tile_rows : (s + 1) * tile_rows] = expd
            run_sum = run_sum + expd
        inv = 1.0 / jnp.sum(run_sum, axis=1, keepdims=True)
        for s in range(max_keys):
            cols = slice(s * tile_rows, (s + 1) * tile_rows)
            pbf_scr[:, cols] = (e_scr[:, cols] * inv).astype(jnp.bfloat16)
        prob_bf = pbf_scr[...]
        out = jnp.dot(prob_bf, vg, preferred_element_type=jnp.float32).astype(jnp.bfloat16)
        og_ref[p, 0] = out
        delta = jnp.sum(g.astype(jnp.float32) * out.astype(jnp.float32), axis=1, keepdims=True)
        dprob = lax.dot_general(g, vg, nt, preferred_element_type=jnp.float32)
        for s in range(max_keys):
            cols = slice(s * tile_rows, (s + 1) * tile_rows)
            prob = e_scr[:, cols] * inv
            ds_scr[:, cols] = (prob * (dprob[:, cols] - delta)).astype(jnp.bfloat16)
        dscore = ds_scr[...]
        dq = jnp.dot(dscore, kg, preferred_element_type=jnp.float32) * scaling
        og_ref[p, 1] = dq.astype(og_ref.dtype)
        dk_g = lax.dot_general(dscore, q, tn, preferred_element_type=jnp.float32) * scaling
        dv_g = lax.dot_general(prob_bf, g, tn, preferred_element_type=jnp.float32)
        for s in range(max_keys):
            slot = slot_ref[p, s]
            acc_scr[slot, 0] += dk_g[s * tile_rows : (s + 1) * tile_rows, :]
            acc_scr[slot, 1] += dv_g[s * tile_rows : (s + 1) * tile_rows, :]
        return carry

    lax.fori_loop(0, query_tiles, body, 0)
    gprev_ref[...] = acc_scr[:query_tiles].astype(gprev_ref.dtype)
    gown_ref[...] = acc_scr[query_tiles : 2 * query_tiles]
    gnext_ref[...] = acc_scr[2 * query_tiles :].astype(gnext_ref.dtype)


def attention_heads(qg, kv_prev, kv_own, kv_next, slot_key, live_slot):
    query_tiles, count, tile_rows, width = qg.shape
    max_keys = slot_key.shape[1]
    head_count = width // HD
    spec = pl.BlockSpec((query_tiles, count, tile_rows, HD), lambda h, *_: (0, 0, 0, h))
    flops = 12 * query_tiles * max_keys * tile_rows * tile_rows * HD * head_count
    grid_spec = pltpu.PrefetchScalarGridSpec(
        num_scalar_prefetch=2,
        grid=(head_count,),
        in_specs=[spec, spec, spec, spec],
        out_specs=[spec, spec, spec, spec],
        scratch_shapes=[
            pltpu.VMEM((max_keys * tile_rows, HD), jnp.bfloat16),
            pltpu.VMEM((max_keys * tile_rows, HD), jnp.bfloat16),
            pltpu.VMEM((3 * query_tiles, count, tile_rows, HD), jnp.float32),
            pltpu.VMEM((tile_rows, max_keys * tile_rows), jnp.float32),
            pltpu.VMEM((tile_rows, max_keys * tile_rows), jnp.bfloat16),
            pltpu.VMEM((tile_rows, max_keys * tile_rows), jnp.bfloat16),
        ],
    )
    block = qg.shape
    return pl.pallas_call(
        attn_kernel,
        grid_spec=grid_spec,
        out_shape=[
            jax.ShapeDtypeStruct(block, jnp.bfloat16),
            jax.ShapeDtypeStruct(block, jnp.float32),
            jax.ShapeDtypeStruct(block, jnp.bfloat16),
            jax.ShapeDtypeStruct(block, jnp.bfloat16),
        ],
        cost_estimate=pl.CostEstimate(
            flops=flops,
            transcendentals=query_tiles * max_keys * tile_rows * tile_rows * head_count,
            bytes_accessed=query_tiles * count * tile_rows * width * 2 * 8,
        ),
    )(slot_key, live_slot.astype(jnp.int32), qg, kv_prev, kv_own, kv_next)


def split_kernel(*refs):
    count = len(refs) - 1
    groups, _, _, part = refs[-1].shape
    for j in range(groups):
        for i in range(count):
            refs[-1][j, i] = refs[i][:, j * part : (j + 1) * part]


def join_kernel(*refs):
    groups, count, _, part = refs[0].shape
    for j in range(groups):
        for i in range(count):
            refs[1 + i][:, j * part : (j + 1) * part] = refs[0][j, i]


def split_columns(arrays, groups):
    rows, width = arrays[0].shape
    part = width // groups
    count = len(arrays)
    return pl.pallas_call(
        split_kernel,
        in_specs=[pl.BlockSpec(memory_space=pltpu.VMEM)] * count,
        out_specs=pl.BlockSpec(memory_space=pltpu.VMEM),
        out_shape=jax.ShapeDtypeStruct((groups, count, rows, part), arrays[0].dtype),
    )(*arrays)


def join_columns(stacked):
    groups, count, rows, part = stacked.shape
    return pl.pallas_call(
        join_kernel,
        in_specs=[pl.BlockSpec(memory_space=pltpu.VMEM)],
        out_specs=[pl.BlockSpec(memory_space=pltpu.VMEM)] * count,
        out_shape=[jax.ShapeDtypeStruct((rows, groups * part), stacked.dtype)] * count,
    )(stacked)


def to_heads(arrays, groups):
    stacked = split_columns(arrays, groups)
    return lax.all_to_all(stacked, "head", split_axis=0, concat_axis=0, tiled=True)


def to_tokens(stacked):
    moved = lax.all_to_all(stacked, "head", split_axis=0, concat_axis=0, tiled=True)
    return join_columns(moved)


def local(query, key, value, grad_out, block_mask, tile_order):
    per_frame = lax.axis_size("head")
    frames = lax.axis_size("tile")
    frame_idx = lax.axis_index("tile")
    max_keys = 3 * min(3, per_frame // 2)
    forward_active, _ = window_lists(block_mask, tile_order, frame_idx, frames, per_frame)
    slot_key, live_slot = compact_slots(forward_active, max_keys)
    kv = to_heads([key, value], per_frame)
    kv_prev = passed_along(kv, "tile", 1)
    kv_next = passed_along(kv, "tile", -1)
    qg = to_heads([query, grad_out], per_frame)
    og, grad_own, grad_prev, grad_next = attention_heads(
        qg, kv_prev, kv, kv_next, slot_key, live_slot
    )
    attn_out, grad_query = to_tokens(og)
    from_above = passed_along(grad_prev, "tile", -1).astype(jnp.float32)
    from_below = passed_along(grad_next, "tile", 1).astype(jnp.float32)
    summed = (grad_own + from_above + from_below).astype(jnp.bfloat16)
    grad_key, grad_value = to_tokens(summed)
    return (attn_out, grad_query, grad_key, grad_value)


def solution(mesh):
    in_specs = (
        P(("tile", "head"), None),
        P(("tile", "head"), None),
        P(("tile", "head"), None),
        P(("tile", "head"), None),
        P(),
        P(),
    )
    out_specs = (
        P(("tile", "head"), None),
        P(("tile", "head"), None),
        P(("tile", "head"), None),
        P(("tile", "head"), None),
    )
    return jax.shard_map(local, mesh=mesh, in_specs=in_specs, out_specs=out_specs, check_vma=False)
```

```python
import jax
import jax.numpy as jnp
from jax import lax
from jax.sharding import PartitionSpec as P
from jax.experimental import pallas as pl
from jax.experimental.pallas import tpu as pltpu

HD = 128


NEG = -1e30


def with_halo(array, sides, width):
    for axis, dim in sides:
        size, length = (lax.axis_size(axis), array.shape[dim])
        up = [(i, (i + 1) % size) for i in range(size - 1)]
        down = [(j, i) for i, j in up]
        last = lax.slice_in_dim(array, length - width, length, axis=dim)
        initial = lax.slice_in_dim(array, 0, width, axis=dim)
        before = lax.ppermute(last, axis, up)
        after = lax.ppermute(initial, axis, down)
        array = jnp.concatenate([before, array, after], axis=dim)
    return array


def passed_along(value, axis, steps):
    count = lax.axis_size(axis)
    initial, last = (max(0, -steps), min(count, count - steps))
    return lax.ppermute(value, axis, [(source, source + steps) for source in range(initial, last)])


def window_lists(block_mask, tile_order, frame_idx, frames, per_frame):
    tile_count = per_frame * frames
    query_clip = lax.dynamic_slice_in_dim(tile_order, frame_idx * per_frame, per_frame)
    cand_slot = (frame_idx - 1) * per_frame + jnp.arange(3 * per_frame, dtype=jnp.int32)
    valid_slot = ((cand_slot >= 0) & (cand_slot < tile_count)).astype(jnp.int32)
    cand_clip = jnp.take(tile_order, jnp.clip(cand_slot, 0, tile_count - 1))
    forward_active = block_mask[query_clip[:, None], cand_clip[None, :]] * valid_slot[None, :]
    backward_active = block_mask[cand_clip[:, None], query_clip[None, :]] * valid_slot[:, None]
    return (forward_active, backward_active)


def compact_slots(forward_active, max_keys):
    slot_key = jnp.argsort(1 - forward_active, axis=1, stable=True)[:, :max_keys]
    live_slot = jnp.take_along_axis(forward_active, slot_key, axis=1) > 0
    return (slot_key, live_slot)


def attn_kernel(
    slot_ref, live_ref, qg_ref, prev_ref, own_ref, next_ref,
    og_ref, gown_ref, gprev_ref, gnext_ref, kg_scr, vg_scr, acc_scr,
):
    tile_rows = HD
    query_tiles, max_keys = slot_ref.shape
    scaling = HD ** (-0.5)
    window = (prev_ref, own_ref, next_ref)
    acc_scr[...] = jnp.zeros(acc_scr.shape, acc_scr.dtype)
    nt = (((1,), (1,)), ((), ()))
    tn = (((0,), (0,)), ((), ()))
    lane_slot = lax.broadcasted_iota(jnp.int32, (1, max_keys * tile_rows), 1) // tile_rows

    def body(p, carry):
        live_lane = jnp.zeros((1, max_keys * tile_rows), jnp.int32)
        for s in range(max_keys):
            slot = slot_ref[p, s]
            side = slot // query_tiles
            tile = slot % query_tiles
            dst = slice(s * tile_rows, (s + 1) * tile_rows)
            for i, buf in ((0, kg_scr), (1, vg_scr)):
                picked = window[0][tile, i]
                for w in (1, 2):
                    picked = jnp.where(side == w, window[w][tile, i], picked)
                buf[dst, :] = picked

            live_lane = jnp.where(lane_slot == s, live_ref[p, s], live_lane)
        q = qg_ref[p, 0]
        g = qg_ref[p, 1]
        kg = kg_scr[...]
        vg = vg_scr[...]
        sc = lax.dot_general(q, kg, nt, preferred_element_type=jnp.float32) * scaling
        sc = jnp.where(live_lane > 0, sc, NEG)
        top = jnp.max(sc, axis=1, keepdims=True)
        expd = jnp.exp(sc - top)
        prob = expd * (1.0 / jnp.sum(expd, axis=1, keepdims=True))
        prob_bf = prob.astype(jnp.bfloat16)
        out = jnp.dot(prob_bf, vg, preferred_element_type=jnp.float32).astype(jnp.bfloat16)
        og_ref[p, 0] = out
        delta = jnp.sum(g.astype(jnp.float32) * out.astype(jnp.float32), axis=1, keepdims=True)
        dprob = lax.dot_general(g, vg, nt, preferred_element_type=jnp.float32)
        dscore = (prob * (dprob - delta)).astype(jnp.bfloat16)
        dq = jnp.dot(dscore, kg, preferred_element_type=jnp.float32) * scaling
        og_ref[p, 1] = dq.astype(og_ref.dtype)
        dk_g = lax.dot_general(dscore, q, tn, preferred_element_type=jnp.float32) * scaling
        dv_g = lax.dot_general(prob_bf, g, tn, preferred_element_type=jnp.float32)
        for s in range(max_keys):
            slot = slot_ref[p, s]
            acc_scr[slot, 0] += dk_g[s * tile_rows : (s + 1) * tile_rows, :]
            acc_scr[slot, 1] += dv_g[s * tile_rows : (s + 1) * tile_rows, :]
        return carry

    lax.fori_loop(0, query_tiles, body, 0, unroll=2)
    gprev_ref[...] = acc_scr[:query_tiles].astype(gprev_ref.dtype)
    gown_ref[...] = acc_scr[query_tiles : 2 * query_tiles]
    gnext_ref[...] = acc_scr[2 * query_tiles :].astype(gnext_ref.dtype)


def attention_heads(qg, kv_prev, kv_own, kv_next, slot_key, live_slot):
    query_tiles, count, tile_rows, width = qg.shape
    max_keys = slot_key.shape[1]
    head_count = width // HD
    spec = pl.BlockSpec((query_tiles, count, tile_rows, HD), lambda h, *_: (0, 0, 0, h))
    flops = 12 * query_tiles * max_keys * tile_rows * tile_rows * HD * head_count
    grid_spec = pltpu.PrefetchScalarGridSpec(
        num_scalar_prefetch=2,
        grid=(head_count,),
        in_specs=[spec, spec, spec, spec],
        out_specs=[spec, spec, spec, spec],
        scratch_shapes=[
            pltpu.VMEM((max_keys * tile_rows, HD), jnp.bfloat16),
            pltpu.VMEM((max_keys * tile_rows, HD), jnp.bfloat16),
            pltpu.VMEM((3 * query_tiles, count, tile_rows, HD), jnp.float32),
        ],
    )
    block = qg.shape
    return pl.pallas_call(
        attn_kernel,
        grid_spec=grid_spec,
        out_shape=[
            jax.ShapeDtypeStruct(block, jnp.bfloat16),
            jax.ShapeDtypeStruct(block, jnp.float32),
            jax.ShapeDtypeStruct(block, jnp.bfloat16),
            jax.ShapeDtypeStruct(block, jnp.bfloat16),
        ],
        cost_estimate=pl.CostEstimate(
            flops=flops,
            transcendentals=query_tiles * max_keys * tile_rows * tile_rows * head_count,
            bytes_accessed=query_tiles * count * tile_rows * width * 2 * 8,
        ),
    )(slot_key, live_slot.astype(jnp.int32), qg, kv_prev, kv_own, kv_next)


def split_kernel(*refs):
    count = len(refs) - 1
    groups, _, _, part = refs[-1].shape
    for j in range(groups):
        for i in range(count):
            refs[-1][j, i] = refs[i][:, j * part : (j + 1) * part]


def join_kernel(*refs):
    groups, count, _, part = refs[0].shape
    for j in range(groups):
        for i in range(count):
            refs[1 + i][:, j * part : (j + 1) * part] = refs[0][j, i]


def split_columns(arrays, groups):
    rows, width = arrays[0].shape
    part = width // groups
    count = len(arrays)
    return pl.pallas_call(
        split_kernel,
        in_specs=[pl.BlockSpec(memory_space=pltpu.VMEM)] * count,
        out_specs=pl.BlockSpec(memory_space=pltpu.VMEM),
        out_shape=jax.ShapeDtypeStruct((groups, count, rows, part), arrays[0].dtype),
    )(*arrays)


def join_columns(stacked):
    groups, count, rows, part = stacked.shape
    return pl.pallas_call(
        join_kernel,
        in_specs=[pl.BlockSpec(memory_space=pltpu.VMEM)],
        out_specs=[pl.BlockSpec(memory_space=pltpu.VMEM)] * count,
        out_shape=[jax.ShapeDtypeStruct((rows, groups * part), stacked.dtype)] * count,
    )(stacked)


def to_heads(arrays, groups):
    stacked = split_columns(arrays, groups)
    return lax.all_to_all(stacked, "head", split_axis=0, concat_axis=0, tiled=True)


def to_tokens(stacked):
    moved = lax.all_to_all(stacked, "head", split_axis=0, concat_axis=0, tiled=True)
    return join_columns(moved)


def local(query, key, value, grad_out, block_mask, tile_order):
    per_frame = lax.axis_size("head")
    frames = lax.axis_size("tile")
    frame_idx = lax.axis_index("tile")
    max_keys = 3 * min(3, per_frame // 2)
    forward_active, _ = window_lists(block_mask, tile_order, frame_idx, frames, per_frame)
    slot_key, live_slot = compact_slots(forward_active, max_keys)
    kv = to_heads([key, value], per_frame)
    kv_prev = passed_along(kv, "tile", 1)
    kv_next = passed_along(kv, "tile", -1)
    qg = to_heads([query, grad_out], per_frame)
    og, grad_own, grad_prev, grad_next = attention_heads(
        qg, kv_prev, kv, kv_next, slot_key, live_slot
    )
    attn_out, grad_query = to_tokens(og)
    from_above = passed_along(grad_prev, "tile", -1).astype(jnp.float32)
    from_below = passed_along(grad_next, "tile", 1).astype(jnp.float32)
    summed = (grad_own + from_above + from_below).astype(jnp.bfloat16)
    grad_key, grad_value = to_tokens(summed)
    return (attn_out, grad_query, grad_key, grad_value)


def solution(mesh):
    in_specs = (
        P(("tile", "head"), None),
        P(("tile", "head"), None),
        P(("tile", "head"), None),
        P(("tile", "head"), None),
        P(),
        P(),
    )
    out_specs = (
        P(("tile", "head"), None),
        P(("tile", "head"), None),
        P(("tile", "head"), None),
        P(("tile", "head"), None),
    )
    return jax.shard_map(local, mesh=mesh, in_specs=in_specs, out_specs=out_specs, check_vma=False)
```

```python
import jax
import jax.numpy as jnp
from jax import lax
from jax.sharding import PartitionSpec as P
from jax.experimental import pallas as pl
from jax.experimental.pallas import tpu as pltpu

HD = 128


NEG = -1e30


def with_halo(array, sides, width):
    for axis, dim in sides:
        size, length = (lax.axis_size(axis), array.shape[dim])
        up = [(i, (i + 1) % size) for i in range(size - 1)]
        down = [(j, i) for i, j in up]
        last = lax.slice_in_dim(array, length - width, length, axis=dim)
        initial = lax.slice_in_dim(array, 0, width, axis=dim)
        before = lax.ppermute(last, axis, up)
        after = lax.ppermute(initial, axis, down)
        array = jnp.concatenate([before, array, after], axis=dim)
    return array


def passed_along(value, axis, steps):
    count = lax.axis_size(axis)
    initial, last = (max(0, -steps), min(count, count - steps))
    return lax.ppermute(value, axis, [(source, source + steps) for source in range(initial, last)])


def window_lists(block_mask, tile_order, frame_idx, frames, per_frame):
    tile_count = per_frame * frames
    query_clip = lax.dynamic_slice_in_dim(tile_order, frame_idx * per_frame, per_frame)
    cand_slot = (frame_idx - 1) * per_frame + jnp.arange(3 * per_frame, dtype=jnp.int32)
    valid_slot = ((cand_slot >= 0) & (cand_slot < tile_count)).astype(jnp.int32)
    cand_clip = jnp.take(tile_order, jnp.clip(cand_slot, 0, tile_count - 1))
    forward_active = block_mask[query_clip[:, None], cand_clip[None, :]] * valid_slot[None, :]
    backward_active = block_mask[cand_clip[:, None], query_clip[None, :]] * valid_slot[:, None]
    return (forward_active, backward_active)


def compact_slots(forward_active, max_keys):
    slot_key = jnp.argsort(1 - forward_active, axis=1, stable=True)[:, :max_keys]
    live_slot = jnp.take_along_axis(forward_active, slot_key, axis=1) > 0
    return (slot_key, live_slot)


def attn_kernel(
    slot_ref, live_ref, qg_ref, kp_ref, ko_ref, kn_ref, vp_ref, vo_ref, vn_ref,
    og_ref, gok_ref, gov_ref, gpk_ref, gpv_ref, gnk_ref, gnv_ref, kg_scr, vg_scr, acc_scr,
):
    tile_rows = HD
    query_tiles, max_keys = slot_ref.shape
    scaling = HD ** (-0.5)
    windows = ((kp_ref, ko_ref, kn_ref), (vp_ref, vo_ref, vn_ref))
    acc_scr[...] = jnp.zeros(acc_scr.shape, acc_scr.dtype)
    nt = (((1,), (1,)), ((), ()))
    tn = (((0,), (0,)), ((), ()))
    lane_slot = lax.broadcasted_iota(jnp.int32, (1, max_keys * tile_rows), 1) // tile_rows

    def body(p, carry):
        live_lane = jnp.zeros((1, max_keys * tile_rows), jnp.int32)
        for s in range(max_keys):
            slot = slot_ref[p, s]
            side = slot // query_tiles
            tile = slot % query_tiles
            dst = slice(s * tile_rows, (s + 1) * tile_rows)
            for window, buf in zip(windows, (kg_scr, vg_scr)):
                picked = window[0][tile, 0]
                for w in (1, 2):
                    picked = jnp.where(side == w, window[w][tile, 0], picked)
                buf[dst, :] = picked

            live_lane = jnp.where(lane_slot == s, live_ref[p, s], live_lane)
        q = qg_ref[p, 0]
        g = qg_ref[p, 1]
        kg = kg_scr[...]
        vg = vg_scr[...]
        sc = lax.dot_general(q, kg, nt, preferred_element_type=jnp.float32) * scaling
        sc = jnp.where(live_lane > 0, sc, NEG)
        top = jnp.max(sc, axis=1, keepdims=True)
        expd = jnp.exp(sc - top)
        prob = expd * (1.0 / jnp.sum(expd, axis=1, keepdims=True))
        prob_bf = prob.astype(jnp.bfloat16)
        out = jnp.dot(prob_bf, vg, preferred_element_type=jnp.float32).astype(jnp.bfloat16)
        og_ref[p, 0] = out
        delta = jnp.sum(g.astype(jnp.float32) * out.astype(jnp.float32), axis=1, keepdims=True)
        dprob = lax.dot_general(g, vg, nt, preferred_element_type=jnp.float32)
        dscore = (prob * (dprob - delta)).astype(jnp.bfloat16)
        dq = jnp.dot(dscore, kg, preferred_element_type=jnp.float32) * scaling
        og_ref[p, 1] = dq.astype(og_ref.dtype)
        dk_g = lax.dot_general(dscore, q, tn, preferred_element_type=jnp.float32) * scaling
        dv_g = lax.dot_general(prob_bf, g, tn, preferred_element_type=jnp.float32)
        for s in range(max_keys):
            slot = slot_ref[p, s]
            acc_scr[slot, 0] += dk_g[s * tile_rows : (s + 1) * tile_rows, :]
            acc_scr[slot, 1] += dv_g[s * tile_rows : (s + 1) * tile_rows, :]
        return carry

    lax.fori_loop(0, query_tiles, body, 0, unroll=2)
    for i, (own, before, after) in enumerate(((gok_ref, gpk_ref, gnk_ref), (gov_ref, gpv_ref, gnv_ref))):
        before[...] = acc_scr[:query_tiles, i : i + 1].astype(before.dtype)
        own[...] = acc_scr[query_tiles : 2 * query_tiles, i : i + 1]
        after[...] = acc_scr[2 * query_tiles :, i : i + 1].astype(after.dtype)


def attention_heads(qg, k_win, v_win, slot_key, live_slot):
    query_tiles, count, tile_rows, width = qg.shape
    max_keys = slot_key.shape[1]
    head_count = width // HD
    spec = pl.BlockSpec((query_tiles, count, tile_rows, HD), lambda h, *_: (0, 0, 0, h))
    one = pl.BlockSpec((query_tiles, 1, tile_rows, HD), lambda h, *_: (0, 0, 0, h))
    second = pl.BlockSpec((query_tiles, 1, tile_rows, HD), lambda h, *_: (0, 1, 0, h))
    flops = 12 * query_tiles * max_keys * tile_rows * tile_rows * HD * head_count
    grid_spec = pltpu.PrefetchScalarGridSpec(
        num_scalar_prefetch=2,
        grid=(head_count,),
        in_specs=[spec] + [one] * 3 + [second] * 3,
        out_specs=[spec] + [one] * 6,
        scratch_shapes=[
            pltpu.VMEM((max_keys * tile_rows, HD), jnp.bfloat16),
            pltpu.VMEM((max_keys * tile_rows, HD), jnp.bfloat16),
            pltpu.VMEM((3 * query_tiles, count, tile_rows, HD), jnp.float32),
        ],
    )
    single = (query_tiles, 1, tile_rows, width)
    return pl.pallas_call(
        attn_kernel,
        grid_spec=grid_spec,
        out_shape=[jax.ShapeDtypeStruct(qg.shape, jnp.bfloat16)]
        + [jax.ShapeDtypeStruct(single, jnp.float32)] * 2
        + [jax.ShapeDtypeStruct(single, jnp.bfloat16)] * 4,
        cost_estimate=pl.CostEstimate(
            flops=flops,
            transcendentals=query_tiles * max_keys * tile_rows * tile_rows * head_count,
            bytes_accessed=query_tiles * count * tile_rows * width * 2 * 8,
        ),
    )(slot_key, live_slot.astype(jnp.int32), qg, *k_win, *v_win)


def split_kernel(*refs):
    count = len(refs) - 1
    groups, _, _, part = refs[-1].shape
    for j in range(groups):
        for i in range(count):
            refs[-1][j, i] = refs[i][:, j * part : (j + 1) * part]


def join_kernel(*refs):
    groups, count, _, part = refs[0].shape
    for j in range(groups):
        for i in range(count):
            refs[1 + i][:, j * part : (j + 1) * part] = refs[0][j, i]


def split_columns(arrays, groups):
    rows, width = arrays[0].shape
    part = width // groups
    count = len(arrays)
    return pl.pallas_call(
        split_kernel,
        in_specs=[pl.BlockSpec(memory_space=pltpu.VMEM)] * count,
        out_specs=pl.BlockSpec(memory_space=pltpu.VMEM),
        out_shape=jax.ShapeDtypeStruct((groups, count, rows, part), arrays[0].dtype),
    )(*arrays)


def join_columns(stacked):
    groups, count, rows, part = stacked.shape
    return pl.pallas_call(
        join_kernel,
        in_specs=[pl.BlockSpec(memory_space=pltpu.VMEM)],
        out_specs=[pl.BlockSpec(memory_space=pltpu.VMEM)] * count,
        out_shape=[jax.ShapeDtypeStruct((rows, groups * part), stacked.dtype)] * count,
    )(stacked)


def to_heads(arrays, groups):
    stacked = split_columns(arrays, groups)
    return lax.all_to_all(stacked, "head", split_axis=0, concat_axis=0, tiled=True)


def to_tokens(stacked):
    moved = lax.all_to_all(stacked, "head", split_axis=0, concat_axis=0, tiled=True)
    return join_columns(moved)


def local(query, key, value, grad_out, block_mask, tile_order):
    per_frame = lax.axis_size("head")
    frames = lax.axis_size("tile")
    frame_idx = lax.axis_index("tile")
    max_keys = 3 * min(3, per_frame // 2)
    forward_active, _ = window_lists(block_mask, tile_order, frame_idx, frames, per_frame)
    slot_key, live_slot = compact_slots(forward_active, max_keys)
    kv = to_heads([key, value], per_frame)
    k_win = (passed_along(kv, "tile", 1), kv, passed_along(kv, "tile", -1))
    v_win = k_win
    qg = to_heads([query, grad_out], per_frame)
    og, gok, gov, gpk, gpv, gnk, gnv = attention_heads(qg, k_win, v_win, slot_key, live_slot)
    attn_out, grad_query = to_tokens(og)
    grads = []
    for own, before, after in ((gok, gpk, gnk), (gov, gpv, gnv)):
        from_above = passed_along(before, "tile", -1).astype(jnp.float32)
        from_below = passed_along(after, "tile", 1).astype(jnp.float32)
        grads.append(to_tokens((own + from_above + from_below).astype(jnp.bfloat16))[0])
    return (attn_out, grad_query, grads[0], grads[1])


def solution(mesh):
    in_specs = (
        P(("tile", "head"), None),
        P(("tile", "head"), None),
        P(("tile", "head"), None),
        P(("tile", "head"), None),
        P(),
        P(),
    )
    out_specs = (
        P(("tile", "head"), None),
        P(("tile", "head"), None),
        P(("tile", "head"), None),
        P(("tile", "head"), None),
    )
    return jax.shard_map(local, mesh=mesh, in_specs=in_specs, out_specs=out_specs, check_vma=False)
```

```python
import jax
import jax.numpy as jnp
from jax import lax
from jax.sharding import PartitionSpec as P
from jax.experimental import pallas as pl
from jax.experimental.pallas import tpu as pltpu

HD = 128


NEG = -1e30


def with_halo(array, sides, width):
    for axis, dim in sides:
        size, length = (lax.axis_size(axis), array.shape[dim])
        up = [(i, (i + 1) % size) for i in range(size - 1)]
        down = [(j, i) for i, j in up]
        last = lax.slice_in_dim(array, length - width, length, axis=dim)
        initial = lax.slice_in_dim(array, 0, width, axis=dim)
        before = lax.ppermute(last, axis, up)
        after = lax.ppermute(initial, axis, down)
        array = jnp.concatenate([before, array, after], axis=dim)
    return array


def passed_along(value, axis, steps):
    count = lax.axis_size(axis)
    initial, last = (max(0, -steps), min(count, count - steps))
    return lax.ppermute(value, axis, [(source, source + steps) for source in range(initial, last)])


def window_lists(block_mask, tile_order, frame_idx, frames, per_frame):
    tile_count = per_frame * frames
    query_clip = lax.dynamic_slice_in_dim(tile_order, frame_idx * per_frame, per_frame)
    cand_slot = (frame_idx - 1) * per_frame + jnp.arange(3 * per_frame, dtype=jnp.int32)
    valid_slot = ((cand_slot >= 0) & (cand_slot < tile_count)).astype(jnp.int32)
    cand_clip = jnp.take(tile_order, jnp.clip(cand_slot, 0, tile_count - 1))
    forward_active = block_mask[query_clip[:, None], cand_clip[None, :]] * valid_slot[None, :]
    backward_active = block_mask[cand_clip[:, None], query_clip[None, :]] * valid_slot[:, None]
    return (forward_active, backward_active)


def compact_slots(forward_active, max_keys):
    slot_key = jnp.argsort(1 - forward_active, axis=1, stable=True)[:, :max_keys]
    live_slot = jnp.take_along_axis(forward_active, slot_key, axis=1) > 0
    return (slot_key, live_slot)


def attn_kernel(
    slot_ref, live_ref, qg_ref, kp_ref, ko_ref, kn_ref, vp_ref, vo_ref, vn_ref,
    og_ref, gok_ref, gov_ref, gpk_ref, gpv_ref, gnk_ref, gnv_ref, kg_scr, vg_scr, acc_scr,
):
    tile_rows = HD
    query_tiles, max_keys = slot_ref.shape
    scaling = HD ** (-0.5)
    windows = ((kp_ref, ko_ref, kn_ref), (vp_ref, vo_ref, vn_ref))
    acc_scr[...] = jnp.zeros(acc_scr.shape, acc_scr.dtype)
    nt = (((1,), (1,)), ((), ()))
    tn = (((0,), (0,)), ((), ()))
    lane_slot = lax.broadcasted_iota(jnp.int32, (1, max_keys * tile_rows), 1) // tile_rows

    def body(p, carry):
        live_lane = jnp.zeros((1, max_keys * tile_rows), jnp.int32)
        for s in range(max_keys):
            slot = slot_ref[p, s]
            side = slot // query_tiles
            tile = slot % query_tiles
            dst = slice(s * tile_rows, (s + 1) * tile_rows)
            for window, buf in zip(windows, (kg_scr, vg_scr)):
                picked = window[0][tile, 0]
                for w in (1, 2):
                    picked = jnp.where(side == w, window[w][tile, 0], picked)
                buf[dst, :] = picked

            live_lane = jnp.where(lane_slot == s, live_ref[p, s], live_lane)
        q = qg_ref[p, 0]
        g = qg_ref[p, 1]
        kg = kg_scr[...]
        vg = vg_scr[...]
        sc = lax.dot_general(q, kg, nt, preferred_element_type=jnp.float32) * scaling
        sc = jnp.where(live_lane > 0, sc, NEG)
        top = jnp.max(sc, axis=1, keepdims=True)
        expd = jnp.exp(sc - top)
        prob = expd * (1.0 / jnp.sum(expd, axis=1, keepdims=True))
        prob_bf = prob.astype(jnp.bfloat16)
        out = jnp.dot(prob_bf, vg, preferred_element_type=jnp.float32).astype(jnp.bfloat16)
        og_ref[p, 0] = out
        delta = jnp.sum(g.astype(jnp.float32) * out.astype(jnp.float32), axis=1, keepdims=True)
        dprob = lax.dot_general(g, vg, nt, preferred_element_type=jnp.float32)
        dscore = (prob * (dprob - delta)).astype(jnp.bfloat16)
        dq = jnp.dot(dscore, kg, preferred_element_type=jnp.float32) * scaling
        og_ref[p, 1] = dq.astype(og_ref.dtype)
        dk_g = lax.dot_general(dscore, q, tn, preferred_element_type=jnp.float32) * scaling
        dv_g = lax.dot_general(prob_bf, g, tn, preferred_element_type=jnp.float32)
        for s in range(max_keys):
            slot = slot_ref[p, s]
            acc_scr[slot, 0] += dk_g[s * tile_rows : (s + 1) * tile_rows, :]
            acc_scr[slot, 1] += dv_g[s * tile_rows : (s + 1) * tile_rows, :]
        return carry

    lax.fori_loop(0, query_tiles, body, 0, unroll=2)
    for i, (own, before, after) in enumerate(((gok_ref, gpk_ref, gnk_ref), (gov_ref, gpv_ref, gnv_ref))):
        before[...] = acc_scr[:query_tiles, i : i + 1].astype(before.dtype)
        own[...] = acc_scr[query_tiles : 2 * query_tiles, i : i + 1].astype(own.dtype)
        after[...] = acc_scr[2 * query_tiles :, i : i + 1].astype(after.dtype)


def attention_heads(qg, k_win, v_win, slot_key, live_slot):
    query_tiles, count, tile_rows, width = qg.shape
    max_keys = slot_key.shape[1]
    head_count = width // HD
    spec = pl.BlockSpec((query_tiles, count, tile_rows, HD), lambda h, *_: (0, 0, 0, h))
    one = pl.BlockSpec((query_tiles, 1, tile_rows, HD), lambda h, *_: (0, 0, 0, h))
    second = pl.BlockSpec((query_tiles, 1, tile_rows, HD), lambda h, *_: (0, 1, 0, h))
    flops = 12 * query_tiles * max_keys * tile_rows * tile_rows * HD * head_count
    grid_spec = pltpu.PrefetchScalarGridSpec(
        num_scalar_prefetch=2,
        grid=(head_count,),
        in_specs=[spec] + [one] * 3 + [second] * 3,
        out_specs=[spec] + [one] * 6,
        scratch_shapes=[
            pltpu.VMEM((max_keys * tile_rows, HD), jnp.bfloat16),
            pltpu.VMEM((max_keys * tile_rows, HD), jnp.bfloat16),
            pltpu.VMEM((3 * query_tiles, count, tile_rows, HD), jnp.float32),
        ],
    )
    single = (query_tiles, 1, tile_rows, width)
    return pl.pallas_call(
        attn_kernel,
        grid_spec=grid_spec,
        out_shape=[jax.ShapeDtypeStruct(qg.shape, jnp.bfloat16)]
        + [jax.ShapeDtypeStruct(single, jnp.bfloat16)] * 6,
        cost_estimate=pl.CostEstimate(
            flops=flops,
            transcendentals=query_tiles * max_keys * tile_rows * tile_rows * head_count,
            bytes_accessed=query_tiles * count * tile_rows * width * 2 * 8,
        ),
    )(slot_key, live_slot.astype(jnp.int32), qg, *k_win, *v_win)


def split_kernel(*refs):
    count = len(refs) - 1
    groups, _, _, part = refs[-1].shape
    for j in range(groups):
        for i in range(count):
            refs[-1][j, i] = refs[i][:, j * part : (j + 1) * part]


def join_kernel(*refs):
    groups, count, _, part = refs[0].shape
    for j in range(groups):
        for i in range(count):
            refs[1 + i][:, j * part : (j + 1) * part] = refs[0][j, i]


def split_columns(arrays, groups, blocks=4):
    rows, width = arrays[0].shape
    part = width // groups
    count = len(arrays)
    step = rows // blocks
    return pl.pallas_call(
        split_kernel,
        grid=(blocks,),
        in_specs=[pl.BlockSpec((step, width), lambda r: (r, 0))] * count,
        out_specs=pl.BlockSpec((groups, count, step, part), lambda r: (0, 0, r, 0)),
        out_shape=jax.ShapeDtypeStruct((groups, count, rows, part), arrays[0].dtype),
    )(*arrays)


def join_columns(stacked, blocks=4):
    groups, count, rows, part = stacked.shape
    step = rows // blocks
    return pl.pallas_call(
        join_kernel,
        grid=(blocks,),
        in_specs=[pl.BlockSpec((groups, count, step, part), lambda r: (0, 0, r, 0))],
        out_specs=[pl.BlockSpec((step, groups * part), lambda r: (r, 0))] * count,
        out_shape=[jax.ShapeDtypeStruct((rows, groups * part), stacked.dtype)] * count,
    )(stacked)


def to_heads(arrays, groups):
    stacked = split_columns(arrays, groups)
    return lax.all_to_all(stacked, "head", split_axis=0, concat_axis=0, tiled=True)


def to_tokens(stacked):
    moved = lax.all_to_all(stacked, "head", split_axis=0, concat_axis=0, tiled=True)
    return join_columns(moved)


def local(query, key, value, grad_out, block_mask, tile_order):
    per_frame = lax.axis_size("head")
    frames = lax.axis_size("tile")
    frame_idx = lax.axis_index("tile")
    max_keys = 3 * min(3, per_frame // 2)
    forward_active, _ = window_lists(block_mask, tile_order, frame_idx, frames, per_frame)
    slot_key, live_slot = compact_slots(forward_active, max_keys)
    kv = to_heads([key, value], per_frame)
    k_win = (passed_along(kv, "tile", 1), kv, passed_along(kv, "tile", -1))
    v_win = k_win
    qg = to_heads([query, grad_out], per_frame)
    og, gok, gov, gpk, gpv, gnk, gnv = attention_heads(qg, k_win, v_win, slot_key, live_slot)
    attn_out, grad_query = to_tokens(og)
    grads = []
    for own, before, after in ((gok, gpk, gnk), (gov, gpv, gnv)):
        from_above = passed_along(before, "tile", -1).astype(jnp.float32)
        from_below = passed_along(after, "tile", 1).astype(jnp.float32)
        summed = own.astype(jnp.float32) + from_above + from_below
        grads.append(to_tokens(summed.astype(jnp.bfloat16))[0])
    return (attn_out, grad_query, grads[0], grads[1])


def solution(mesh):
    in_specs = (
        P(("tile", "head"), None),
        P(("tile", "head"), None),
        P(("tile", "head"), None),
        P(("tile", "head"), None),
        P(),
        P(),
    )
    out_specs = (
        P(("tile", "head"), None),
        P(("tile", "head"), None),
        P(("tile", "head"), None),
        P(("tile", "head"), None),
    )
    return jax.shard_map(local, mesh=mesh, in_specs=in_specs, out_specs=out_specs, check_vma=False)
```

```python
import jax
import jax.numpy as jnp
from jax import lax
from jax.sharding import PartitionSpec as P
from jax.experimental import pallas as pl
from jax.experimental.pallas import tpu as pltpu

HD = 128


NEG = -1e30


def with_halo(array, sides, width):
    for axis, dim in sides:
        size, length = (lax.axis_size(axis), array.shape[dim])
        up = [(i, (i + 1) % size) for i in range(size - 1)]
        down = [(j, i) for i, j in up]
        last = lax.slice_in_dim(array, length - width, length, axis=dim)
        initial = lax.slice_in_dim(array, 0, width, axis=dim)
        before = lax.ppermute(last, axis, up)
        after = lax.ppermute(initial, axis, down)
        array = jnp.concatenate([before, array, after], axis=dim)
    return array


def passed_along(value, axis, steps):
    count = lax.axis_size(axis)
    initial, last = (max(0, -steps), min(count, count - steps))
    return lax.ppermute(value, axis, [(source, source + steps) for source in range(initial, last)])


def window_lists(block_mask, tile_order, frame_idx, frames, per_frame):
    tile_count = per_frame * frames
    query_clip = lax.dynamic_slice_in_dim(tile_order, frame_idx * per_frame, per_frame)
    cand_slot = (frame_idx - 1) * per_frame + jnp.arange(3 * per_frame, dtype=jnp.int32)
    valid_slot = ((cand_slot >= 0) & (cand_slot < tile_count)).astype(jnp.int32)
    cand_clip = jnp.take(tile_order, jnp.clip(cand_slot, 0, tile_count - 1))
    forward_active = block_mask[query_clip[:, None], cand_clip[None, :]] * valid_slot[None, :]
    backward_active = block_mask[cand_clip[:, None], query_clip[None, :]] * valid_slot[:, None]
    return (forward_active, backward_active)


def compact_slots(forward_active, max_keys):
    slot_key = jnp.argsort(1 - forward_active, axis=1, stable=True)[:, :max_keys]
    live_slot = jnp.take_along_axis(forward_active, slot_key, axis=1) > 0
    return (slot_key, live_slot)


def attn_kernel(
    slot_ref, live_ref, gather_ref, qg_ref, kp_ref, ko_ref, kn_ref, vp_ref, vo_ref, vn_ref,
    og_ref, gok_ref, gov_ref, gpk_ref, gpv_ref, gnk_ref, gnv_ref, kg_scr, vg_scr, acc_scr,
):
    tile_rows = HD
    query_tiles, max_keys = slot_ref.shape
    scaling = HD ** (-0.5)
    windows = ((kp_ref, ko_ref, kn_ref), (vp_ref, vo_ref, vn_ref))
    acc_scr[...] = jnp.zeros(acc_scr.shape, acc_scr.dtype)
    nt = (((1,), (1,)), ((), ()))
    tn = (((0,), (0,)), ((), ()))
    lane_slot = lax.broadcasted_iota(jnp.int32, (1, max_keys * tile_rows), 1) // tile_rows

    def body(p, carry):
        live_lane = jnp.zeros((1, max_keys * tile_rows), jnp.int32)
        for s in range(max_keys):
            slot = gather_ref[p, s]
            side = slot // query_tiles
            tile = slot % query_tiles
            dst = slice(s * tile_rows, (s + 1) * tile_rows)
            for window, buf in zip(windows, (kg_scr, vg_scr)):
                picked = window[0][tile, 0]
                for w in (1, 2):
                    picked = jnp.where(side == w, window[w][tile, 0], picked)
                buf[dst, :] = picked

            live_lane = jnp.where(lane_slot == s, live_ref[p, s], live_lane)
        q = qg_ref[p, 0]
        g = qg_ref[p, 1]
        kg = kg_scr[...]
        vg = vg_scr[...]
        sc = lax.dot_general(q, kg, nt, preferred_element_type=jnp.float32) * scaling
        sc = jnp.where(live_lane > 0, sc, NEG)
        top = jnp.max(sc, axis=1, keepdims=True)
        expd = jnp.exp(sc - top)
        prob = expd * (1.0 / jnp.sum(expd, axis=1, keepdims=True))
        prob_bf = prob.astype(jnp.bfloat16)
        out = jnp.dot(prob_bf, vg, preferred_element_type=jnp.float32).astype(jnp.bfloat16)
        og_ref[p, 0] = out
        delta = jnp.sum(g.astype(jnp.float32) * out.astype(jnp.float32), axis=1, keepdims=True)
        dprob = lax.dot_general(g, vg, nt, preferred_element_type=jnp.float32)
        dscore = (prob * (dprob - delta)).astype(jnp.bfloat16)
        dq = jnp.dot(dscore, kg, preferred_element_type=jnp.float32) * scaling
        og_ref[p, 1] = dq.astype(og_ref.dtype)
        dk_g = lax.dot_general(dscore, q, tn, preferred_element_type=jnp.float32) * scaling
        dv_g = lax.dot_general(prob_bf, g, tn, preferred_element_type=jnp.float32)
        for s in range(max_keys):
            slot = slot_ref[p, s]
            acc_scr[slot, 0] += dk_g[s * tile_rows : (s + 1) * tile_rows, :]
            acc_scr[slot, 1] += dv_g[s * tile_rows : (s + 1) * tile_rows, :]
        return carry

    lax.fori_loop(0, query_tiles, body, 0, unroll=2)
    for i, (own, before, after) in enumerate(((gok_ref, gpk_ref, gnk_ref), (gov_ref, gpv_ref, gnv_ref))):
        before[...] = acc_scr[:query_tiles, i : i + 1].astype(before.dtype)
        own[...] = acc_scr[query_tiles : 2 * query_tiles, i : i + 1]
        after[...] = acc_scr[2 * query_tiles :, i : i + 1].astype(after.dtype)


def attention_heads(qg, k_win, v_win, slot_key, live_slot, gather_key):
    query_tiles, count, tile_rows, width = qg.shape
    max_keys = slot_key.shape[1]
    head_count = width // HD
    spec = pl.BlockSpec((query_tiles, count, tile_rows, HD), lambda h, *_: (0, 0, 0, h))
    one = pl.BlockSpec((query_tiles, 1, tile_rows, HD), lambda h, *_: (0, 0, 0, h))
    second = pl.BlockSpec((query_tiles, 1, tile_rows, HD), lambda h, *_: (0, 1, 0, h))
    flops = 12 * query_tiles * max_keys * tile_rows * tile_rows * HD * head_count
    grid_spec = pltpu.PrefetchScalarGridSpec(
        num_scalar_prefetch=3,
        grid=(head_count,),
        in_specs=[spec] + [one] * 3 + [second] * 3,
        out_specs=[spec] + [one] * 6,
        scratch_shapes=[
            pltpu.VMEM((max_keys * tile_rows, HD), jnp.bfloat16),
            pltpu.VMEM((max_keys * tile_rows, HD), jnp.bfloat16),
            pltpu.VMEM((3 * query_tiles, count, tile_rows, HD), jnp.float32),
        ],
    )
    single = (query_tiles, 1, tile_rows, width)
    return pl.pallas_call(
        attn_kernel,
        grid_spec=grid_spec,
        out_shape=[jax.ShapeDtypeStruct(qg.shape, jnp.bfloat16)]
        + [jax.ShapeDtypeStruct(single, jnp.float32)] * 2
        + [jax.ShapeDtypeStruct(single, jnp.bfloat16)] * 4,
        cost_estimate=pl.CostEstimate(
            flops=flops,
            transcendentals=query_tiles * max_keys * tile_rows * tile_rows * head_count,
            bytes_accessed=query_tiles * count * tile_rows * width * 2 * 8,
        ),
    )(slot_key, live_slot.astype(jnp.int32), gather_key, qg, *k_win, *v_win)


def split_kernel(*refs):
    count = len(refs) - 1
    groups, _, _, part = refs[-1].shape
    for j in range(groups):
        for i in range(count):
            refs[-1][j, i] = refs[i][:, j * part : (j + 1) * part]


def join_kernel(*refs):
    groups, count, _, part = refs[0].shape
    for j in range(groups):
        for i in range(count):
            refs[1 + i][:, j * part : (j + 1) * part] = refs[0][j, i]


def split_columns(arrays, groups):
    rows, width = arrays[0].shape
    part = width // groups
    count = len(arrays)
    return pl.pallas_call(
        split_kernel,
        in_specs=[pl.BlockSpec(memory_space=pltpu.VMEM)] * count,
        out_specs=pl.BlockSpec(memory_space=pltpu.VMEM),
        out_shape=jax.ShapeDtypeStruct((groups, count, rows, part), arrays[0].dtype),
    )(*arrays)


def join_columns(stacked):
    groups, count, rows, part = stacked.shape
    return pl.pallas_call(
        join_kernel,
        in_specs=[pl.BlockSpec(memory_space=pltpu.VMEM)],
        out_specs=[pl.BlockSpec(memory_space=pltpu.VMEM)] * count,
        out_shape=[jax.ShapeDtypeStruct((rows, groups * part), stacked.dtype)] * count,
    )(stacked)


def to_heads(arrays, groups):
    stacked = split_columns(arrays, groups)
    return lax.all_to_all(stacked, "head", split_axis=0, concat_axis=0, tiled=True)


def to_tokens(stacked):
    moved = lax.all_to_all(stacked, "head", split_axis=0, concat_axis=0, tiled=True)
    return join_columns(moved)


def exchange_heads(arrays, groups):
    stacked = split_columns(arrays, groups)
    me = lax.axis_index("head")
    received = [lax.dynamic_index_in_dim(stacked, me, keepdims=False)]
    for shift in range(1, groups):
        block = lax.dynamic_index_in_dim(stacked, (me + shift) % groups, keepdims=False)
        pairs = [(j, (j + shift) % groups) for j in range(groups)]
        received.append(lax.ppermute(block, "head", pairs))
    return jnp.stack(received)


def local(query, key, value, grad_out, block_mask, tile_order):
    per_frame = lax.axis_size("head")
    frames = lax.axis_size("tile")
    frame_idx = lax.axis_index("tile")
    max_keys = 3 * min(3, per_frame // 2)
    forward_active, _ = window_lists(block_mask, tile_order, frame_idx, frames, per_frame)
    slot_key, live_slot = compact_slots(forward_active, max_keys)
    kv = exchange_heads([key, value], per_frame)
    me = lax.axis_index("head")
    side, tile = slot_key // per_frame, slot_key % per_frame
    gather_key = (side * per_frame + (me - tile) % per_frame).astype(jnp.int32)
    kv, query, grad_out = lax.optimization_barrier((kv, query, grad_out))
    k_win = (passed_along(kv, "tile", 1), kv, passed_along(kv, "tile", -1))
    v_win = k_win
    qg = to_heads([query, grad_out], per_frame)
    og, gok, gov, gpk, gpv, gnk, gnv = attention_heads(qg, k_win, v_win, slot_key, live_slot, gather_key)
    attn_out, grad_query = to_tokens(og)
    grads = []
    for own, before, after in ((gok, gpk, gnk), (gov, gpv, gnv)):
        from_above = passed_along(before, "tile", -1).astype(jnp.float32)
        from_below = passed_along(after, "tile", 1).astype(jnp.float32)
        grads.append(to_tokens((own + from_above + from_below).astype(jnp.bfloat16))[0])
    return (attn_out, grad_query, grads[0], grads[1])


def solution(mesh):
    in_specs = (
        P(("tile", "head"), None),
        P(("tile", "head"), None),
        P(("tile", "head"), None),
        P(("tile", "head"), None),
        P(),
        P(),
    )
    out_specs = (
        P(("tile", "head"), None),
        P(("tile", "head"), None),
        P(("tile", "head"), None),
        P(("tile", "head"), None),
    )
    return jax.shard_map(local, mesh=mesh, in_specs=in_specs, out_specs=out_specs, check_vma=False)
```

```python
import jax
import jax.numpy as jnp
from jax import lax
from jax.sharding import PartitionSpec as P
from jax.experimental import pallas as pl
from jax.experimental.pallas import tpu as pltpu

HD = 128


NEG = -1e30


def with_halo(array, sides, width):
    for axis, dim in sides:
        size, length = (lax.axis_size(axis), array.shape[dim])
        up = [(i, (i + 1) % size) for i in range(size - 1)]
        down = [(j, i) for i, j in up]
        last = lax.slice_in_dim(array, length - width, length, axis=dim)
        initial = lax.slice_in_dim(array, 0, width, axis=dim)
        before = lax.ppermute(last, axis, up)
        after = lax.ppermute(initial, axis, down)
        array = jnp.concatenate([before, array, after], axis=dim)
    return array


def passed_along(value, axis, steps):
    count = lax.axis_size(axis)
    initial, last = (max(0, -steps), min(count, count - steps))
    return lax.ppermute(value, axis, [(source, source + steps) for source in range(initial, last)])


def window_lists(block_mask, tile_order, frame_idx, frames, per_frame):
    tile_count = per_frame * frames
    query_clip = lax.dynamic_slice_in_dim(tile_order, frame_idx * per_frame, per_frame)
    cand_slot = (frame_idx - 1) * per_frame + jnp.arange(3 * per_frame, dtype=jnp.int32)
    valid_slot = ((cand_slot >= 0) & (cand_slot < tile_count)).astype(jnp.int32)
    cand_clip = jnp.take(tile_order, jnp.clip(cand_slot, 0, tile_count - 1))
    forward_active = block_mask[query_clip[:, None], cand_clip[None, :]] * valid_slot[None, :]
    backward_active = block_mask[cand_clip[:, None], query_clip[None, :]] * valid_slot[:, None]
    return (forward_active, backward_active)


def compact_slots(forward_active, max_keys):
    slot_key = jnp.argsort(1 - forward_active, axis=1, stable=True)[:, :max_keys]
    live_slot = jnp.take_along_axis(forward_active, slot_key, axis=1) > 0
    return (slot_key, live_slot)


def attn_kernel(
    slot_ref, live_ref, qg_ref, kp_ref, ko_ref, kn_ref, vp_ref, vo_ref, vn_ref,
    og_ref, gok_ref, gov_ref, gpk_ref, gpv_ref, gnk_ref, gnv_ref, kg_scr, vg_scr, acc_scr,
):
    tile_rows = HD
    query_tiles, max_keys = slot_ref.shape
    scaling = HD ** (-0.5)
    windows = ((kp_ref, ko_ref, kn_ref), (vp_ref, vo_ref, vn_ref))
    acc_scr[...] = jnp.zeros(acc_scr.shape, acc_scr.dtype)
    nt = (((1,), (1,)), ((), ()))
    tn = (((0,), (0,)), ((), ()))
    lane_slot = lax.broadcasted_iota(jnp.int32, (1, max_keys * tile_rows), 1) // tile_rows

    def body(p, carry):
        live_lane = jnp.zeros((1, max_keys * tile_rows), jnp.int32)
        for s in range(max_keys):
            slot = slot_ref[p, s]
            side = slot // query_tiles
            tile = slot % query_tiles
            dst = slice(s * tile_rows, (s + 1) * tile_rows)
            for window, buf in zip(windows, (kg_scr, vg_scr)):
                picked = window[0][tile, 0]
                for w in (1, 2):
                    picked = jnp.where(side == w, window[w][tile, 0], picked)
                buf[dst, :] = picked

            live_lane = jnp.where(lane_slot == s, live_ref[p, s], live_lane)
        q = qg_ref[p, 0]
        g = qg_ref[p, 1]
        kg = kg_scr[...]
        vg = vg_scr[...]
        sc = lax.dot_general(q, kg, nt, preferred_element_type=jnp.float32)
        sc = jnp.where(live_lane > 0, sc, NEG)
        top = jnp.max(sc, axis=1, keepdims=True)
        expd = jnp.exp((sc - top) * scaling)
        prob = expd * (1.0 / jnp.sum(expd, axis=1, keepdims=True))
        prob_bf = prob.astype(jnp.bfloat16)
        out = jnp.dot(prob_bf, vg, preferred_element_type=jnp.float32).astype(jnp.bfloat16)
        og_ref[p, 0] = out
        delta = jnp.sum(g.astype(jnp.float32) * out.astype(jnp.float32), axis=1, keepdims=True)
        dprob = lax.dot_general(g, vg, nt, preferred_element_type=jnp.float32)
        dscore = (prob * (dprob - delta)).astype(jnp.bfloat16)
        dq = jnp.dot(dscore, kg, preferred_element_type=jnp.float32) * scaling
        og_ref[p, 1] = dq.astype(og_ref.dtype)
        dk_g = lax.dot_general(dscore, q, tn, preferred_element_type=jnp.float32) * scaling
        dv_g = lax.dot_general(prob_bf, g, tn, preferred_element_type=jnp.float32)
        for s in range(max_keys):
            slot = slot_ref[p, s]
            acc_scr[slot, 0] += dk_g[s * tile_rows : (s + 1) * tile_rows, :]
            acc_scr[slot, 1] += dv_g[s * tile_rows : (s + 1) * tile_rows, :]
        return carry

    lax.fori_loop(0, query_tiles, body, 0, unroll=2)
    for i, (own, before, after) in enumerate(((gok_ref, gpk_ref, gnk_ref), (gov_ref, gpv_ref, gnv_ref))):
        before[...] = acc_scr[:query_tiles, i : i + 1].astype(before.dtype)
        own[...] = acc_scr[query_tiles : 2 * query_tiles, i : i + 1]
        after[...] = acc_scr[2 * query_tiles :, i : i + 1].astype(after.dtype)


def attention_heads(qg, k_win, v_win, slot_key, live_slot):
    query_tiles, count, tile_rows, width = qg.shape
    max_keys = slot_key.shape[1]
    head_count = width // HD
    spec = pl.BlockSpec((query_tiles, count, tile_rows, HD), lambda h, *_: (0, 0, 0, h))
    one = pl.BlockSpec((query_tiles, 1, tile_rows, HD), lambda h, *_: (0, 0, 0, h))
    second = pl.BlockSpec((query_tiles, 1, tile_rows, HD), lambda h, *_: (0, 1, 0, h))
    flops = 12 * query_tiles * max_keys * tile_rows * tile_rows * HD * head_count
    grid_spec = pltpu.PrefetchScalarGridSpec(
        num_scalar_prefetch=2,
        grid=(head_count,),
        in_specs=[spec] + [one] * 3 + [second] * 3,
        out_specs=[spec] + [one] * 6,
        scratch_shapes=[
            pltpu.VMEM((max_keys * tile_rows, HD), jnp.bfloat16),
            pltpu.VMEM((max_keys * tile_rows, HD), jnp.bfloat16),
            pltpu.VMEM((3 * query_tiles, count, tile_rows, HD), jnp.float32),
        ],
    )
    single = (query_tiles, 1, tile_rows, width)
    return pl.pallas_call(
        attn_kernel,
        grid_spec=grid_spec,
        out_shape=[jax.ShapeDtypeStruct(qg.shape, jnp.bfloat16)]
        + [jax.ShapeDtypeStruct(single, jnp.float32)] * 2
        + [jax.ShapeDtypeStruct(single, jnp.bfloat16)] * 4,
        cost_estimate=pl.CostEstimate(
            flops=flops,
            transcendentals=query_tiles * max_keys * tile_rows * tile_rows * head_count,
            bytes_accessed=query_tiles * count * tile_rows * width * 2 * 8,
        ),
    )(slot_key, live_slot.astype(jnp.int32), qg, *k_win, *v_win)


def split_kernel(*refs):
    count = len(refs) - 1
    groups, _, _, part = refs[-1].shape
    for j in range(groups):
        for i in range(count):
            refs[-1][j, i] = refs[i][:, j * part : (j + 1) * part]


def join_kernel(*refs):
    groups, count, _, part = refs[0].shape
    for j in range(groups):
        for i in range(count):
            refs[1 + i][:, j * part : (j + 1) * part] = refs[0][j, i]


def split_columns(arrays, groups):
    rows, width = arrays[0].shape
    part = width // groups
    count = len(arrays)
    return pl.pallas_call(
        split_kernel,
        in_specs=[pl.BlockSpec(memory_space=pltpu.VMEM)] * count,
        out_specs=pl.BlockSpec(memory_space=pltpu.VMEM),
        out_shape=jax.ShapeDtypeStruct((groups, count, rows, part), arrays[0].dtype),
    )(*arrays)


def join_columns(stacked):
    groups, count, rows, part = stacked.shape
    return pl.pallas_call(
        join_kernel,
        in_specs=[pl.BlockSpec(memory_space=pltpu.VMEM)],
        out_specs=[pl.BlockSpec(memory_space=pltpu.VMEM)] * count,
        out_shape=[jax.ShapeDtypeStruct((rows, groups * part), stacked.dtype)] * count,
    )(stacked)


def to_heads(arrays, groups):
    stacked = split_columns(arrays, groups)
    return lax.all_to_all(stacked, "head", split_axis=0, concat_axis=0, tiled=True)


def to_tokens(stacked):
    moved = lax.all_to_all(stacked, "head", split_axis=0, concat_axis=0, tiled=True)
    return join_columns(moved)


def local(query, key, value, grad_out, block_mask, tile_order):
    per_frame = lax.axis_size("head")
    frames = lax.axis_size("tile")
    frame_idx = lax.axis_index("tile")
    max_keys = 3 * min(3, per_frame // 2)
    forward_active, _ = window_lists(block_mask, tile_order, frame_idx, frames, per_frame)
    slot_key, live_slot = compact_slots(forward_active, max_keys)
    kv = to_heads([key, value], per_frame)
    k_win = (passed_along(kv, "tile", 1), kv, passed_along(kv, "tile", -1))
    v_win = k_win
    qg = to_heads([query, grad_out], per_frame)
    og, gok, gov, gpk, gpv, gnk, gnv = attention_heads(qg, k_win, v_win, slot_key, live_slot)
    attn_out, grad_query = to_tokens(og)
    grads = []
    for own, before, after in ((gok, gpk, gnk), (gov, gpv, gnv)):
        from_above = passed_along(before, "tile", -1).astype(jnp.float32)
        from_below = passed_along(after, "tile", 1).astype(jnp.float32)
        grads.append(to_tokens((own + from_above + from_below).astype(jnp.bfloat16))[0])
    return (attn_out, grad_query, grads[0], grads[1])


def solution(mesh):
    in_specs = (
        P(("tile", "head"), None),
        P(("tile", "head"), None),
        P(("tile", "head"), None),
        P(("tile", "head"), None),
        P(),
        P(),
    )
    out_specs = (
        P(("tile", "head"), None),
        P(("tile", "head"), None),
        P(("tile", "head"), None),
        P(("tile", "head"), None),
    )
    return jax.shard_map(local, mesh=mesh, in_specs=in_specs, out_specs=out_specs, check_vma=False)
```

```python
import jax
import jax.numpy as jnp
from jax import lax
from jax.sharding import PartitionSpec as P
from jax.experimental import pallas as pl
from jax.experimental.pallas import tpu as pltpu

HD = 128


NEG = -1e30


def with_halo(array, sides, width):
    for axis, dim in sides:
        size, length = (lax.axis_size(axis), array.shape[dim])
        up = [(i, (i + 1) % size) for i in range(size - 1)]
        down = [(j, i) for i, j in up]
        last = lax.slice_in_dim(array, length - width, length, axis=dim)
        initial = lax.slice_in_dim(array, 0, width, axis=dim)
        before = lax.ppermute(last, axis, up)
        after = lax.ppermute(initial, axis, down)
        array = jnp.concatenate([before, array, after], axis=dim)
    return array


def passed_along(value, axis, steps):
    count = lax.axis_size(axis)
    initial, last = (max(0, -steps), min(count, count - steps))
    return lax.ppermute(value, axis, [(source, source + steps) for source in range(initial, last)])


def window_lists(block_mask, tile_order, frame_idx, frames, per_frame):
    tile_count = per_frame * frames
    query_clip = lax.dynamic_slice_in_dim(tile_order, frame_idx * per_frame, per_frame)
    cand_slot = (frame_idx - 1) * per_frame + jnp.arange(3 * per_frame, dtype=jnp.int32)
    valid_slot = ((cand_slot >= 0) & (cand_slot < tile_count)).astype(jnp.int32)
    cand_clip = jnp.take(tile_order, jnp.clip(cand_slot, 0, tile_count - 1))
    forward_active = block_mask[query_clip[:, None], cand_clip[None, :]] * valid_slot[None, :]
    backward_active = block_mask[cand_clip[:, None], query_clip[None, :]] * valid_slot[:, None]
    return (forward_active, backward_active)


def compact_slots(forward_active, max_keys):
    slot_key = jnp.argsort(1 - forward_active, axis=1, stable=True)[:, :max_keys]
    live_slot = jnp.take_along_axis(forward_active, slot_key, axis=1) > 0
    return (slot_key, live_slot)


def attn_kernel(
    slot_ref, live_ref, qg_ref, kp_ref, ko_ref, kn_ref, vp_ref, vo_ref, vn_ref,
    og_ref, gok_ref, gov_ref, gpk_ref, gpv_ref, gnk_ref, gnv_ref, kg_scr, vg_scr, acc_scr,
):
    tile_rows = HD
    query_tiles, max_keys = slot_ref.shape
    scaling = HD ** (-0.5)
    windows = ((kp_ref, ko_ref, kn_ref), (vp_ref, vo_ref, vn_ref))
    acc_scr[...] = jnp.zeros(acc_scr.shape, acc_scr.dtype)
    nt = (((1,), (1,)), ((), ()))
    tn = (((0,), (0,)), ((), ()))
    lane_slot = lax.broadcasted_iota(jnp.int32, (1, max_keys * tile_rows), 1) // tile_rows

    def body(p, carry):
        live_lane = jnp.zeros((1, max_keys * tile_rows), jnp.int32)
        for s in range(max_keys):
            slot = slot_ref[p, s]
            side = slot // query_tiles
            tile = slot % query_tiles
            dst = slice(s * tile_rows, (s + 1) * tile_rows)
            for window, buf in zip(windows, (kg_scr, vg_scr)):
                picked = window[0][tile, 0]
                for w in (1, 2):
                    picked = jnp.where(side == w, window[w][tile, 0], picked)
                buf[dst, :] = picked

            live_lane = jnp.where(lane_slot == s, live_ref[p, s], live_lane)
        q = qg_ref[p, 0]
        g = qg_ref[p, 1]
        kg = kg_scr[...]
        vg = vg_scr[...]
        sc = lax.dot_general(q, kg, nt, preferred_element_type=jnp.float32) * scaling
        sc = jnp.where(live_lane > 0, sc, NEG)
        top = jnp.max(sc, axis=1, keepdims=True)
        expd = jnp.exp(sc - top)
        prob = expd * (1.0 / jnp.sum(expd, axis=1, keepdims=True))
        prob_bf = prob.astype(jnp.bfloat16)
        out = jnp.dot(prob_bf, vg, preferred_element_type=jnp.float32).astype(jnp.bfloat16)
        og_ref[p, 0] = out
        delta = jnp.sum(g.astype(jnp.float32) * out.astype(jnp.float32), axis=1, keepdims=True)
        dprob = lax.dot_general(g, vg, nt, preferred_element_type=jnp.float32)
        dscore = (prob * (dprob - delta)).astype(jnp.bfloat16)
        dq = jnp.dot(dscore, kg, preferred_element_type=jnp.float32) * scaling
        og_ref[p, 1] = dq.astype(og_ref.dtype)
        dk_g = lax.dot_general(dscore, q, tn, preferred_element_type=jnp.float32) * scaling
        dv_g = lax.dot_general(prob_bf, g, tn, preferred_element_type=jnp.float32)
        for s in range(max_keys):
            slot = slot_ref[p, s]
            acc_scr[slot, 0] += dk_g[s * tile_rows : (s + 1) * tile_rows, :]
            acc_scr[slot, 1] += dv_g[s * tile_rows : (s + 1) * tile_rows, :]
        return carry

    lax.fori_loop(0, query_tiles, body, 0, unroll=2)
    for i, (own, before, after) in enumerate(((gok_ref, gpk_ref, gnk_ref), (gov_ref, gpv_ref, gnv_ref))):
        before[...] = acc_scr[:query_tiles, i : i + 1].astype(before.dtype)
        own[...] = acc_scr[query_tiles : 2 * query_tiles, i : i + 1].astype(own.dtype)
        after[...] = acc_scr[2 * query_tiles :, i : i + 1].astype(after.dtype)


def attention_heads(qg, k_win, v_win, slot_key, live_slot):
    query_tiles, count, tile_rows, width = qg.shape
    max_keys = slot_key.shape[1]
    head_count = width // HD
    spec = pl.BlockSpec((query_tiles, count, tile_rows, HD), lambda h, *_: (0, 0, 0, h))
    one = pl.BlockSpec((query_tiles, 1, tile_rows, HD), lambda h, *_: (0, 0, 0, h))
    second = pl.BlockSpec((query_tiles, 1, tile_rows, HD), lambda h, *_: (0, 1, 0, h))
    flops = 12 * query_tiles * max_keys * tile_rows * tile_rows * HD * head_count
    grid_spec = pltpu.PrefetchScalarGridSpec(
        num_scalar_prefetch=2,
        grid=(head_count,),
        in_specs=[spec] + [one] * 3 + [second] * 3,
        out_specs=[spec] + [one] * 6,
        scratch_shapes=[
            pltpu.VMEM((max_keys * tile_rows, HD), jnp.bfloat16),
            pltpu.VMEM((max_keys * tile_rows, HD), jnp.bfloat16),
            pltpu.VMEM((3 * query_tiles, count, tile_rows, HD), jnp.float32),
        ],
    )
    single = (query_tiles, 1, tile_rows, width)
    return pl.pallas_call(
        attn_kernel,
        grid_spec=grid_spec,
        out_shape=[jax.ShapeDtypeStruct(qg.shape, jnp.bfloat16)]
        + [jax.ShapeDtypeStruct(single, jnp.bfloat16)] * 6,
        cost_estimate=pl.CostEstimate(
            flops=flops,
            transcendentals=query_tiles * max_keys * tile_rows * tile_rows * head_count,
            bytes_accessed=query_tiles * count * tile_rows * width * 2 * 8,
        ),
    )(slot_key, live_slot.astype(jnp.int32), qg, *k_win, *v_win)


def split_kernel(*refs):
    count = len(refs) - 1
    groups, _, _, part = refs[-1].shape
    for j in range(groups):
        for i in range(count):
            refs[-1][j, i] = refs[i][:, j * part : (j + 1) * part]


def join_kernel(*refs):
    groups, count, _, part = refs[0].shape
    for j in range(groups):
        for i in range(count):
            refs[1 + i][:, j * part : (j + 1) * part] = refs[0][j, i]


def split_columns(arrays, groups):
    rows, width = arrays[0].shape
    part = width // groups
    count = len(arrays)
    return pl.pallas_call(
        split_kernel,
        in_specs=[pl.BlockSpec(memory_space=pltpu.VMEM)] * count,
        out_specs=pl.BlockSpec(memory_space=pltpu.VMEM),
        out_shape=jax.ShapeDtypeStruct((groups, count, rows, part), arrays[0].dtype),
    )(*arrays)


def join_columns(stacked):
    groups, count, rows, part = stacked.shape
    return pl.pallas_call(
        join_kernel,
        in_specs=[pl.BlockSpec(memory_space=pltpu.VMEM)],
        out_specs=[pl.BlockSpec(memory_space=pltpu.VMEM)] * count,
        out_shape=[jax.ShapeDtypeStruct((rows, groups * part), stacked.dtype)] * count,
    )(stacked)


def to_heads(arrays, groups):
    stacked = split_columns(arrays, groups)
    return lax.all_to_all(stacked, "head", split_axis=0, concat_axis=0, tiled=True)


def to_tokens(stacked):
    moved = lax.all_to_all(stacked, "head", split_axis=0, concat_axis=0, tiled=True)
    return join_columns(moved)


def local(query, key, value, grad_out, block_mask, tile_order):
    per_frame = lax.axis_size("head")
    frames = lax.axis_size("tile")
    frame_idx = lax.axis_index("tile")
    max_keys = 3 * min(3, per_frame // 2)
    forward_active, _ = window_lists(block_mask, tile_order, frame_idx, frames, per_frame)
    slot_key, live_slot = compact_slots(forward_active, max_keys)
    kv = to_heads([key, value], per_frame)
    k_win = (passed_along(kv, "tile", 1), kv, passed_along(kv, "tile", -1))
    v_win = k_win
    qg = to_heads([query, grad_out], per_frame)
    og, gok, gov, gpk, gpv, gnk, gnv = attention_heads(qg, k_win, v_win, slot_key, live_slot)
    attn_out, grad_query = to_tokens(og)
    grads = []
    for own, before, after in ((gok, gpk, gnk), (gov, gpv, gnv)):
        from_above = passed_along(before, "tile", -1).astype(jnp.float32)
        from_below = passed_along(after, "tile", 1).astype(jnp.float32)
        summed = own.astype(jnp.float32) + from_above + from_below
        grads.append(to_tokens(summed.astype(jnp.bfloat16))[0])
    return (attn_out, grad_query, grads[0], grads[1])


def solution(mesh):
    in_specs = (
        P(("tile", "head"), None),
        P(("tile", "head"), None),
        P(("tile", "head"), None),
        P(("tile", "head"), None),
        P(),
        P(),
    )
    out_specs = (
        P(("tile", "head"), None),
        P(("tile", "head"), None),
        P(("tile", "head"), None),
        P(("tile", "head"), None),
    )
    return jax.shard_map(local, mesh=mesh, in_specs=in_specs, out_specs=out_specs, check_vma=False)
```

```python
import jax
import jax.numpy as jnp
from jax import lax
from jax.sharding import PartitionSpec as P
from jax.experimental import pallas as pl
from jax.experimental.pallas import tpu as pltpu

HD = 128


NEG = -1e30


def with_halo(array, sides, width):
    for axis, dim in sides:
        size, length = (lax.axis_size(axis), array.shape[dim])
        up = [(i, (i + 1) % size) for i in range(size - 1)]
        down = [(j, i) for i, j in up]
        last = lax.slice_in_dim(array, length - width, length, axis=dim)
        initial = lax.slice_in_dim(array, 0, width, axis=dim)
        before = lax.ppermute(last, axis, up)
        after = lax.ppermute(initial, axis, down)
        array = jnp.concatenate([before, array, after], axis=dim)
    return array


def passed_along(value, axis, steps):
    count = lax.axis_size(axis)
    initial, last = (max(0, -steps), min(count, count - steps))
    return lax.ppermute(value, axis, [(source, source + steps) for source in range(initial, last)])


def window_lists(block_mask, tile_order, frame_idx, frames, per_frame):
    tile_count = per_frame * frames
    query_clip = lax.dynamic_slice_in_dim(tile_order, frame_idx * per_frame, per_frame)
    cand_slot = (frame_idx - 1) * per_frame + jnp.arange(3 * per_frame, dtype=jnp.int32)
    valid_slot = ((cand_slot >= 0) & (cand_slot < tile_count)).astype(jnp.int32)
    cand_clip = jnp.take(tile_order, jnp.clip(cand_slot, 0, tile_count - 1))
    forward_active = block_mask[query_clip[:, None], cand_clip[None, :]] * valid_slot[None, :]
    backward_active = block_mask[cand_clip[:, None], query_clip[None, :]] * valid_slot[:, None]
    return (forward_active, backward_active)


def compact_slots(forward_active, max_keys):
    slot_key = jnp.argsort(1 - forward_active, axis=1, stable=True)[:, :max_keys]
    live_slot = jnp.take_along_axis(forward_active, slot_key, axis=1) > 0
    return (slot_key, live_slot)


def attn_kernel(
    slot_ref, live_ref, bias_ref, qg_ref, kp_ref, ko_ref, kn_ref, vp_ref, vo_ref, vn_ref,
    og_ref, gok_ref, gov_ref, gpk_ref, gpv_ref, gnk_ref, gnv_ref, kg_scr, vg_scr, acc_scr,
):
    tile_rows = HD
    query_tiles, max_keys = slot_ref.shape
    scaling = HD ** (-0.5)
    windows = ((kp_ref, ko_ref, kn_ref), (vp_ref, vo_ref, vn_ref))
    acc_scr[...] = jnp.zeros(acc_scr.shape, acc_scr.dtype)
    nt = (((1,), (1,)), ((), ()))
    tn = (((0,), (0,)), ((), ()))

    def body(p, carry):
        for s in range(max_keys):
            slot = slot_ref[p, s]
            side = slot // query_tiles
            tile = slot % query_tiles
            dst = slice(s * tile_rows, (s + 1) * tile_rows)
            for window, buf in zip(windows, (kg_scr, vg_scr)):
                picked = window[0][tile, 0]
                for w in (1, 2):
                    picked = jnp.where(side == w, window[w][tile, 0], picked)
                buf[dst, :] = picked

        q = qg_ref[p, 0]
        g = qg_ref[p, 1]
        kg = kg_scr[...]
        vg = vg_scr[...]
        sc = lax.dot_general(q, kg, nt, preferred_element_type=jnp.float32) * scaling
        sc = sc + bias_ref[p]
        top = jnp.max(sc, axis=1, keepdims=True)
        expd = jnp.exp(sc - top)
        prob = expd * (1.0 / jnp.sum(expd, axis=1, keepdims=True))
        prob_bf = prob.astype(jnp.bfloat16)
        out = jnp.dot(prob_bf, vg, preferred_element_type=jnp.float32).astype(jnp.bfloat16)
        og_ref[p, 0] = out
        delta = jnp.sum(g.astype(jnp.float32) * out.astype(jnp.float32), axis=1, keepdims=True)
        dprob = lax.dot_general(g, vg, nt, preferred_element_type=jnp.float32)
        dscore = (prob * (dprob - delta)).astype(jnp.bfloat16)
        dq = jnp.dot(dscore, kg, preferred_element_type=jnp.float32) * scaling
        og_ref[p, 1] = dq.astype(og_ref.dtype)
        dk_g = lax.dot_general(dscore, q, tn, preferred_element_type=jnp.float32) * scaling
        dv_g = lax.dot_general(prob_bf, g, tn, preferred_element_type=jnp.float32)
        for s in range(max_keys):
            slot = slot_ref[p, s]
            acc_scr[slot, 0] += dk_g[s * tile_rows : (s + 1) * tile_rows, :]
            acc_scr[slot, 1] += dv_g[s * tile_rows : (s + 1) * tile_rows, :]
        return carry

    lax.fori_loop(0, query_tiles, body, 0, unroll=2)
    for i, (own, before, after) in enumerate(((gok_ref, gpk_ref, gnk_ref), (gov_ref, gpv_ref, gnv_ref))):
        before[...] = acc_scr[:query_tiles, i : i + 1].astype(before.dtype)
        own[...] = acc_scr[query_tiles : 2 * query_tiles, i : i + 1].astype(own.dtype)
        after[...] = acc_scr[2 * query_tiles :, i : i + 1].astype(after.dtype)


def attention_heads(qg, k_win, v_win, slot_key, live_slot):
    query_tiles, count, tile_rows, width = qg.shape
    max_keys = slot_key.shape[1]
    head_count = width // HD
    spec = pl.BlockSpec((query_tiles, count, tile_rows, HD), lambda h, *_: (0, 0, 0, h))
    one = pl.BlockSpec((query_tiles, 1, tile_rows, HD), lambda h, *_: (0, 0, 0, h))
    second = pl.BlockSpec((query_tiles, 1, tile_rows, HD), lambda h, *_: (0, 1, 0, h))
    flops = 12 * query_tiles * max_keys * tile_rows * tile_rows * HD * head_count
    grid_spec = pltpu.PrefetchScalarGridSpec(
        num_scalar_prefetch=2,
        grid=(head_count,),
        in_specs=[pl.BlockSpec((query_tiles, 1, max_keys * tile_rows), lambda h, *_: (0, 0, 0))]
        + [spec] + [one] * 3 + [second] * 3,
        out_specs=[spec] + [one] * 6,
        scratch_shapes=[
            pltpu.VMEM((max_keys * tile_rows, HD), jnp.bfloat16),
            pltpu.VMEM((max_keys * tile_rows, HD), jnp.bfloat16),
            pltpu.VMEM((3 * query_tiles, count, tile_rows, HD), jnp.float32),
        ],
    )
    single = (query_tiles, 1, tile_rows, width)
    bias = jnp.where(live_slot, 0.0, NEG).astype(jnp.float32)
    bias = jnp.repeat(bias, tile_rows, axis=1).reshape(query_tiles, 1, max_keys * tile_rows)
    return pl.pallas_call(
        attn_kernel,
        grid_spec=grid_spec,
        out_shape=[jax.ShapeDtypeStruct(qg.shape, jnp.bfloat16)]
        + [jax.ShapeDtypeStruct(single, jnp.bfloat16)] * 6,
        cost_estimate=pl.CostEstimate(
            flops=flops,
            transcendentals=query_tiles * max_keys * tile_rows * tile_rows * head_count,
            bytes_accessed=query_tiles * count * tile_rows * width * 2 * 8,
        ),
    )(slot_key, live_slot.astype(jnp.int32), bias, qg, *k_win, *v_win)


def split_kernel(*refs):
    count = len(refs) - 1
    groups, _, _, part = refs[-1].shape
    for j in range(groups):
        for i in range(count):
            refs[-1][j, i] = refs[i][:, j * part : (j + 1) * part]


def join_kernel(*refs):
    groups, count, _, part = refs[0].shape
    for j in range(groups):
        for i in range(count):
            refs[1 + i][:, j * part : (j + 1) * part] = refs[0][j, i]


def split_columns(arrays, groups):
    rows, width = arrays[0].shape
    part = width // groups
    count = len(arrays)
    return pl.pallas_call(
        split_kernel,
        in_specs=[pl.BlockSpec(memory_space=pltpu.VMEM)] * count,
        out_specs=pl.BlockSpec(memory_space=pltpu.VMEM),
        out_shape=jax.ShapeDtypeStruct((groups, count, rows, part), arrays[0].dtype),
    )(*arrays)


def join_columns(stacked):
    groups, count, rows, part = stacked.shape
    return pl.pallas_call(
        join_kernel,
        in_specs=[pl.BlockSpec(memory_space=pltpu.VMEM)],
        out_specs=[pl.BlockSpec(memory_space=pltpu.VMEM)] * count,
        out_shape=[jax.ShapeDtypeStruct((rows, groups * part), stacked.dtype)] * count,
    )(stacked)


def to_heads(arrays, groups):
    stacked = split_columns(arrays, groups)
    return lax.all_to_all(stacked, "head", split_axis=0, concat_axis=0, tiled=True)


def to_tokens(stacked):
    moved = lax.all_to_all(stacked, "head", split_axis=0, concat_axis=0, tiled=True)
    return join_columns(moved)


def local(query, key, value, grad_out, block_mask, tile_order):
    per_frame = lax.axis_size("head")
    frames = lax.axis_size("tile")
    frame_idx = lax.axis_index("tile")
    max_keys = 3 * min(3, per_frame // 2)
    forward_active, _ = window_lists(block_mask, tile_order, frame_idx, frames, per_frame)
    slot_key, live_slot = compact_slots(forward_active, max_keys)
    kv = to_heads([key, value], per_frame)
    k_win = (passed_along(kv, "tile", 1), kv, passed_along(kv, "tile", -1))
    v_win = k_win
    qg = to_heads([query, grad_out], per_frame)
    og, gok, gov, gpk, gpv, gnk, gnv = attention_heads(qg, k_win, v_win, slot_key, live_slot)
    attn_out, grad_query = to_tokens(og)
    grads = []
    for own, before, after in ((gok, gpk, gnk), (gov, gpv, gnv)):
        from_above = passed_along(before, "tile", -1).astype(jnp.float32)
        from_below = passed_along(after, "tile", 1).astype(jnp.float32)
        summed = own.astype(jnp.float32) + from_above + from_below
        grads.append(to_tokens(summed.astype(jnp.bfloat16))[0])
    return (attn_out, grad_query, grads[0], grads[1])


def solution(mesh):
    in_specs = (
        P(("tile", "head"), None),
        P(("tile", "head"), None),
        P(("tile", "head"), None),
        P(("tile", "head"), None),
        P(),
        P(),
    )
    out_specs = (
        P(("tile", "head"), None),
        P(("tile", "head"), None),
        P(("tile", "head"), None),
        P(("tile", "head"), None),
    )
    return jax.shard_map(local, mesh=mesh, in_specs=in_specs, out_specs=out_specs, check_vma=False)
```
